128 devices in a mesh: req: 8 (over z, core), exp: 16 (over x, y).
Axes of the slice: x: 4, y: 4, z: 4, core: 2. Of those that a mesh axis runs over, the one named last changes fastest.
Arguments:
- tokens: bfloat16 [32768, 1536], P(('req', 'exp')), may hold values from -6 to 6
- attn_gain: float32 [1536], replicated, may hold values from 0.1 to 1.9
- w_query: bfloat16 [1536, 1536], P('req'), may hold values from -0.15625 to 0.15625
- key_projection: bfloat16 [1536, 256], P('req'), may hold values from -0.15625 to 0.15625
- value_projection: bfloat16 [1536, 256], P('req'), may hold values from -0.15625 to 0.15625
- w_out: bfloat16 [1536, 1536], P(None, 'req'), may hold values from -0.15625 to 0.15625
- moe_gain: float32 [1536], replicated, may hold values from 0.1 to 1.9
- w_gate: bfloat16 [32, 1536, 768], P('exp'), may hold values from -0.15625 to 0.15625
- w_up: bfloat16 [32, 1536, 768], P('exp'), may hold values from -0.15625 to 0.15625
- w_down: bfloat16 [32, 768, 1536], P('exp'), may hold values from -0.21875 to 0.21875
- routes: int32 [32768, 4], P(('req', 'exp')), may hold values from 0 to 31, all different within a row; in each aligned block of 128 rows (0 to 127, 128 to 255, ...) at most 24 rows name the same one
- gate_weights: float32 [32768, 4], P(('req', 'exp')), may hold values from 0.1 to 1
- kv_cache: bfloat16 [512, 1024, 512], P(('req', 'exp')), may hold values from -360 to 360, as said below
- lengths: int32 [512], P(('req', 'exp')), may hold values from 128 to 1024, as said below
- parents: int32 [512, 64], P(('req', 'exp')), may hold values from 0 to 62, as said below
- accepted: int32 [512], P(('req', 'exp')), may hold values from 0 to 63
Outputs:
- layer_out: bfloat16 [32768, 1536], P(('req', 'exp'))
- new_entries: bfloat16 [512, 64, 512], P(('req', 'exp'))
The draws below stay inside these ranges and needn't reach their ends.
Inputs may be any that keep to these rules, and one draw needn't show every extreme that they name: `routes`: each row names 4 different experts; among the rows of one aligned block of 128 rows no expert is named more than 24 times, and in some block one expert exactly 24 times. `kv_cache`: cache entries are finite; slots at or after a request's length hold arbitrary values. `lengths`: some request has exactly 1024 live slots. parents[r, 0] = 0 marks the root; for i >= 1, parents[r, i] < i.
All inputs are finite; a program needn't handle non-finite values.
Results may differ from the reference program's by a relative error of at most 0.013.
The reference program's roundings to bfloat16 on the way count: a program that leaves them out, or rounds other values in their place, can miss the bound.
Values may be sent and summed in bfloat16 or wider, within the bound.
No kernel may reach another device: no remote copies, remote signals or barrier semaphores. Data moves between devices by JAX's collectives and lax.ppermute only.
A program may use at most 128 MiB of HBM per device.

```python
import math
import jax
import jax.numpy as jnp
import numpy as np
from jax import lax

MODEL_WIDTH = 1536
QUERY_HEADS = 12
KEY_VALUE_HEADS = 2
HEAD_SIZE = 128
EXPERTS = 32
FF = 768
TOP = 4
DRAFT_TOKENS = 64
CACHE_SLOTS = 1024
TOK_DEV = 256
REQUEST_COUNT = 512
TOKENS = 32768
CAP = 24


def draw_kv_cache(key, part):
    leading = jax.random.fold_in(key, 0)
    layer_width = 2 * KEY_VALUE_HEADS * HEAD_SIZE
    entries = jnp.clip(jax.random.normal(leading, (REQUEST_COUNT, CACHE_SLOTS, layer_width), jnp.float32), -4.0, 4.0)
    return entries.astype(jnp.bfloat16)


def draw_lengths(key, part):
    values_drawn = jax.random.randint(key, (REQUEST_COUNT,), CACHE_SLOTS // 8, CACHE_SLOTS + 1, dtype=jnp.int32)
    return values_drawn.at[0].set(CACHE_SLOTS)


def draw_parents(key, part):
    upper = jnp.maximum(jnp.arange(DRAFT_TOKENS, dtype=jnp.int32), 1)
    values_drawn = jax.random.randint(key, (REQUEST_COUNT, DRAFT_TOKENS), 0, upper[None, :], dtype=jnp.int32)
    return values_drawn.at[0, DRAFT_TOKENS - 1].set(DRAFT_TOKENS - 2)


def set_ends(result, own_key, least, top_value):
    extent = result.shape
    place = [jax.random.randint(jax.random.fold_in(own_key, axis), (), 0, extent[axis]) for axis in range(len(extent))]
    result = result.at[tuple(place)].set(least)
    longest = extent.index(max(extent))
    place[longest] = (place[longest] + 1) % extent[longest]
    return result.at[tuple(place)].set(top_value)


def level_of(rng, extent, cuts, low, high):
    def one(position, blocks):
        heights = jax.random.uniform(jax.random.fold_in(jax.random.fold_in(rng, 6), position), (blocks,), jnp.float32, low / len(cuts), high / len(cuts))
        return jnp.repeat(jnp.exp(heights), extent[position] // blocks).reshape((-1,) + (1,) * (len(extent) - position - 1))

    gain = one(*cuts[0])
    for cut in cuts[1:]:
        gain = gain * one(*cut)
    return gain


def shared_out(own_key, own, number, rows, count, top, bound, lean):
    sequence = jax.random.permutation(own_key, count)
    heavy_load, usual = load_shares(count, rows * top, bound, lean, True), load_shares(count, rows * top, bound, lean, False)
    places = jnp.arange(count)

    def named(sizes, turn):
        used = int((sizes > 0).sum())
        fixed = max(1, used // 4)
        passed = fixed + (places - fixed + turn * (used - fixed)) % max(1, count - fixed)
        return jnp.zeros((count,), jnp.int32).at[sequence[jnp.where(places < fixed, places, passed)]].set(jnp.asarray(sizes, jnp.int32))

    sizes = jnp.where(number % 4 == 0, named(heavy_load, number // 4), named(usual, number - number // 4 - 1))
    mixed = jax.random.permutation(jax.random.fold_in(own, 3), count)
    donor, receiver = mixed[0:count // 2 * 2:2], mixed[1:count // 2 * 2:2]
    room = jnp.minimum(sizes[donor] - 1, bound - sizes[receiver]) // 2
    room = jnp.where((donor == sequence[0]) | (receiver == sequence[0]) | (sizes[receiver] == 0), 0, jnp.maximum(room, 0))
    passed = jax.random.randint(jax.random.fold_in(own, 4), (count // 2,), 0, 1 << 20) % (room + 1)
    sizes = sizes.at[donor].add(-passed).at[receiver].add(passed)
    items = jnp.searchsorted(jnp.cumsum(sizes), jnp.arange(rows * top), side="right").astype(jnp.int32)
    listing = items.reshape(top, rows).T
    listing = listing[jax.random.permutation(jax.random.fold_in(own, 1), rows)]
    turn = jax.random.randint(jax.random.fold_in(own, 2), (rows, 1), 0, top)
    return jnp.take_along_axis(listing, (jnp.arange(top)[None, :] + turn) % top, axis=1)


def load_shares(amount, total, reach, slope, full):
    portions = [(1 << 20) // math.isqrt(grade ** slope) + 1 for grade in range(1, amount + 1)]
    largest = reach if full else min(reach, max(-(-total // amount), total * portions[0] // sum(portions)))
    least = 1 if total - largest >= amount - 1 else 0
    holding, surplus = [largest] + [least] * (amount - 1), total - largest - least * (amount - 1)
    while surplus > 0:
        movable = [i for i in range(1, amount) if holding[i] < largest] or [i for i in range(1, amount) if holding[i] < reach]
        pool, remaining = sum([portions[i] for i in movable]), surplus
        for i in movable:
            extra = min(reach - holding[i], max(1, remaining * portions[i] // pool), surplus)
            holding[i] = holding[i] + extra
            surplus = surplus - extra
    return np.array(holding)


def gaussian(key, extent, scale, limit, shards=(), kind=jnp.bfloat16):
    values = jax.random.normal(key, extent, jnp.float32) * scale
    if len(shards) > 0:
        values = level_of(key, extent, shards, -0.22, 0.18) * values
    return jnp.clip(values, min=-limit, max=limit).astype(kind)


def setup_inputs(seed: int = 0) -> dict:
    arg_keys = jax.random.split(jax.random.key(seed), 17)
    tokens = gaussian(arg_keys[0], (TOKENS, MODEL_WIDTH), 1.0, 6.0, ((0, 128),))
    attn_gain = jnp.clip(1.0 + 0.18 * jax.random.normal(arg_keys[1], (MODEL_WIDTH,), jnp.float32), 0.1, 1.9)
    w_query = gaussian(arg_keys[2], (MODEL_WIDTH, QUERY_HEADS * HEAD_SIZE), MODEL_WIDTH ** -0.5, 0.15625, ((0, 8),))
    key_projection = gaussian(arg_keys[3], (MODEL_WIDTH, KEY_VALUE_HEADS * HEAD_SIZE), MODEL_WIDTH ** -0.5, 0.15625, ((0, 8),))
    value_projection = gaussian(arg_keys[4], (MODEL_WIDTH, KEY_VALUE_HEADS * HEAD_SIZE), MODEL_WIDTH ** -0.5, 0.15625, ((0, 8),))
    w_out = gaussian(arg_keys[5], (QUERY_HEADS * HEAD_SIZE, MODEL_WIDTH), (QUERY_HEADS * HEAD_SIZE) ** -0.5, 0.15625, ((1, 8),))
    moe_gain = jnp.clip(1.0 + 0.18 * jax.random.normal(arg_keys[6], (MODEL_WIDTH,), jnp.float32), 0.1, 1.9)
    w_gate = gaussian(arg_keys[7], (EXPERTS, MODEL_WIDTH, FF), MODEL_WIDTH ** -0.5, 0.15625, ((0, 16),))
    w_up = gaussian(arg_keys[8], (EXPERTS, MODEL_WIDTH, FF), MODEL_WIDTH ** -0.5, 0.15625, ((0, 16),))
    w_down = gaussian(arg_keys[9], (EXPERTS, FF, MODEL_WIDTH), FF ** -0.5, 0.21875, ((0, 16),))
    routes_keys = jax.random.split(jax.random.fold_in(arg_keys[10], 1), TOKENS // (TOK_DEV // 2))
    routes_turns = jax.random.permutation(jax.random.fold_in(arg_keys[10], 3), TOKENS // (TOK_DEV // 2))
    routes = jax.vmap(lambda own, number: shared_out(jax.random.fold_in(arg_keys[10], 2), own, number, TOK_DEV // 2, EXPERTS, TOP, CAP, 2))(routes_keys, routes_turns).reshape((TOKENS, TOP))
    gate_weights = jnp.clip(jnp.exp(math.log(1.0) - 2.3025851 * jax.random.uniform(arg_keys[11], (TOKENS, TOP), jnp.float32) ** level_of(arg_keys[11], (TOKENS, TOP), ((0, 128),), -0.2, 0.2)), 0.1, 1.0)
    kv_cache = draw_kv_cache(jax.random.fold_in(arg_keys[16], 71), 0)
    lengths = draw_lengths(jax.random.fold_in(arg_keys[16], 71), 0)
    parents = draw_parents(jax.random.fold_in(arg_keys[16], 71), 0)
    accepted = set_ends(jax.random.randint(arg_keys[15], (REQUEST_COUNT,), 0, DRAFT_TOKENS), jax.random.fold_in(arg_keys[15], 1), 0, DRAFT_TOKENS - 1).astype(jnp.int32)
    return dict(tokens=tokens, attn_gain=attn_gain, w_query=w_query, key_projection=key_projection, value_projection=value_projection, w_out=w_out, moe_gain=moe_gain, w_gate=w_gate, w_up=w_up, w_down=w_down, routes=routes, gate_weights=gate_weights, kv_cache=kv_cache, lengths=lengths, parents=parents, accepted=accepted)


eps_norm = 1e-06
rope_base = 1000000.0

def rms_scale(token_rows, gain_vec):
    widened = token_rows.astype(jnp.float32)
    inverse = lax.rsqrt(lax.optimization_barrier(jnp.mean(widened * widened, axis=-1, keepdims=True)) + eps_norm)
    return (widened * inverse * gain_vec.astype(jnp.float32)).astype(jnp.bfloat16)

def rotate(values, positions):
    row_count = values.shape[0]
    head_count = values.shape[1] // HEAD_SIZE
    half_size = HEAD_SIZE // 2
    reshaped_rows = values.reshape(row_count, head_count, HEAD_SIZE)
    frequency = rope_base ** (-jnp.arange(half_size, dtype=jnp.float32) / half_size)
    angles = positions.astype(jnp.float32)[:, None] * frequency[None, :]
    cosine = jnp.cos(angles)[:, None, :]
    sine_part = jnp.sin(angles)[:, None, :]
    leading = reshaped_rows[..., :half_size]
    second = reshaped_rows[..., half_size:]
    turned = jnp.concatenate([leading * cosine - second * sine_part, second * cosine + leading * sine_part], axis=-1)
    return turned.reshape(row_count, head_count * HEAD_SIZE)

def ancestry(parents):
    node_count = parents.shape[-1]
    node_index = jnp.arange(node_count, dtype=jnp.int32)
    parent_step = (parents[..., :, None] == node_index[None, None, :]).astype(jnp.float32)
    closure = jnp.maximum(parent_step, jnp.eye(node_count, dtype=jnp.float32)[None])
    for squaring in range(max(1, (node_count - 1).bit_length())):
        closure = jnp.minimum(jnp.einsum('rij,rjk->rik', closure, closure), 1.0)
    tree_depth = lax.optimization_barrier(jnp.sum(closure, axis=-1)).astype(jnp.int32) - 1
    return (closure, tree_depth)

def attend(query_rows, tree_key_value, cached_row_block, length, closure):
    tree_drafts = query_rows.shape[0]
    queries_per_group = QUERY_HEADS // KEY_VALUE_HEADS
    key_value_width = KEY_VALUE_HEADS * HEAD_SIZE
    reshaped_rows = query_rows.astype(jnp.float32).reshape(tree_drafts, KEY_VALUE_HEADS, queries_per_group, HEAD_SIZE)
    cached_key_rows = cached_row_block[:, :key_value_width].astype(jnp.float32).reshape(-1, KEY_VALUE_HEADS, HEAD_SIZE)
    cached_value_rows = cached_row_block[:, key_value_width:].astype(jnp.float32).reshape(-1, KEY_VALUE_HEADS, HEAD_SIZE)
    tree_key_rows = tree_key_value[:, :key_value_width].astype(jnp.float32).reshape(-1, KEY_VALUE_HEADS, HEAD_SIZE)
    tree_value_rows = tree_key_value[:, key_value_width:].astype(jnp.float32).reshape(-1, KEY_VALUE_HEADS, HEAD_SIZE)
    scale = 1.0 / math.sqrt(HEAD_SIZE)
    cache_scores = jnp.einsum('igsd,jgd->gsij', reshaped_rows, cached_key_rows) * scale
    draft_scores = jnp.einsum('igsd,jgd->gsij', reshaped_rows, tree_key_rows) * scale
    live_cache = (jnp.arange(cached_row_block.shape[0]) < length)[None, None, None, :]
    live_draft = (closure > 0.5)[None, None, :, :]
    cache_scores = jnp.where(live_cache, cache_scores, -1e+30)
    draft_scores = jnp.where(live_draft, draft_scores, -1e+30)
    highest = jnp.maximum(lax.optimization_barrier(jnp.max(cache_scores, axis=-1)), lax.optimization_barrier(jnp.max(draft_scores, axis=-1)))[..., None]
    cache_weight = jnp.exp(cache_scores - highest)
    draft_weight = jnp.exp(draft_scores - highest)
    running = lax.optimization_barrier(jnp.sum(cache_weight, axis=-1, keepdims=True)) + lax.optimization_barrier(jnp.sum(draft_weight, axis=-1, keepdims=True))
    cache_probs = (cache_weight / running).astype(jnp.bfloat16).astype(jnp.float32)
    draft_probs = (draft_weight / running).astype(jnp.bfloat16).astype(jnp.float32)
    context = jnp.einsum('gsij,jgd->igsd', cache_probs, cached_value_rows) + jnp.einsum('gsij,jgd->igsd', draft_probs, tree_value_rows)
    return context.reshape(tree_drafts, QUERY_HEADS * HEAD_SIZE).astype(jnp.bfloat16)

def compact(kv_rows, closure, tree_depth, accepted):
    path_mask = jnp.take_along_axis(closure, accepted[:, None, None].astype(jnp.int32), axis=1)[:, 0, :]
    level = jnp.arange(kv_rows.shape[1], dtype=jnp.int32)
    select = path_mask[:, None, :] * (tree_depth[:, None, :] == level[None, :, None]).astype(jnp.float32)
    return jnp.einsum('rtj,rjw->rtw', select, kv_rows.astype(jnp.float32)).astype(jnp.bfloat16)

def reference(tokens, attn_gain, w_query, key_projection, value_projection, w_out, moe_gain, w_gate, w_up, w_down, routes, gate_weights, kv_cache, lengths, parents, accepted):
    normed = rms_scale(tokens, attn_gain)
    closure, tree_depth = ancestry(parents)
    positions = (lengths[:, None] + tree_depth).reshape(-1)
    query_sum = jnp.dot(normed, w_query, preferred_element_type=jnp.float32)
    key_sum = jnp.dot(normed, key_projection, preferred_element_type=jnp.float32)
    value_sum = jnp.dot(normed, value_projection, preferred_element_type=jnp.float32)
    query_rows = rotate(query_sum, positions).astype(jnp.bfloat16)
    tree_key_value = jnp.concatenate([rotate(key_sum, positions), value_sum], axis=1).astype(jnp.bfloat16)
    query_req = query_rows.reshape(REQUEST_COUNT, DRAFT_TOKENS, QUERY_HEADS * HEAD_SIZE)
    key_value_request = tree_key_value.reshape(REQUEST_COUNT, DRAFT_TOKENS, 2 * KEY_VALUE_HEADS * HEAD_SIZE)

    def one_request(packed):
        return attend(packed[0], packed[1], packed[2], packed[3], packed[4])
    context = lax.map(one_request, (query_req, key_value_request, kv_cache, lengths, closure)).reshape(TOKENS, QUERY_HEADS * HEAD_SIZE)
    attn_out = jnp.dot(context, w_out, preferred_element_type=jnp.float32)
    residual = (tokens.astype(jnp.float32) + attn_out).astype(jnp.bfloat16)
    moe_in = rms_scale(residual, moe_gain)
    flat_expert = routes.reshape(-1)
    owner = jnp.arange(flat_expert.shape[0], dtype=jnp.int32) // TOP
    flat_gate = gate_weights.reshape(-1).astype(jnp.float32)
    row_bound = 2 * TOKENS * TOP // EXPERTS

    def one_expert(summed, packed):
        expert, gate_mat, up_mat, down_mat = packed
        selected_slots = flat_expert == expert
        pair_index = jnp.nonzero(selected_slots, size=row_bound, fill_value=0)[0].astype(jnp.int32)
        live_pair = (jnp.arange(row_bound, dtype=jnp.int32) < jnp.sum(selected_slots.astype(jnp.int32))).astype(jnp.float32)
        token_index = owner[pair_index]
        picked = moe_in[token_index]
        gate_part = jnp.dot(picked, gate_mat, preferred_element_type=jnp.float32)
        up_part = jnp.dot(picked, up_mat, preferred_element_type=jnp.float32)
        hidden = (jnp.maximum(gate_part, 0.0) * up_part).astype(jnp.bfloat16)
        produced = jnp.dot(hidden, down_mat, preferred_element_type=jnp.float32).astype(jnp.bfloat16)
        weighted = produced.astype(jnp.float32) * (flat_gate[pair_index] * live_pair)[:, None]
        return (summed.at[token_index].add(weighted), None)
    start_sum = jnp.zeros((TOKENS, MODEL_WIDTH), jnp.float32)
    expert_ids = jnp.arange(EXPERTS, dtype=jnp.int32)
    mixed, unused = lax.scan(one_expert, start_sum, (expert_ids, w_gate, w_up, w_down))
    layer_out = (residual.astype(jnp.float32) + mixed).astype(jnp.bfloat16)
    new_entries = compact(key_value_request, closure, tree_depth, accepted)
    return (layer_out, new_entries)
```

```python
import math

import jax
import jax.numpy as jnp
from jax import lax
from jax.sharding import PartitionSpec as P

QUERY_HEADS = 12
KEY_VALUE_HEADS = 2
HEAD_SIZE = 128
EXPERTS = 32
TOP = 4
DRAFT_TOKENS = 64
CAP = 24


eps_norm = 1e-06
rope_base = 1000000.0


def rms_scale(token_rows, gain_vec):
    widened = token_rows.astype(jnp.float32)
    inverse = lax.rsqrt(jnp.mean(widened * widened, axis=-1, keepdims=True) + eps_norm)
    return (widened * inverse * gain_vec).astype(jnp.bfloat16)


def rotate(values, positions):
    row_count = values.shape[0]
    head_count = values.shape[1] // HEAD_SIZE
    half_size = HEAD_SIZE // 2
    reshaped_rows = values.reshape(row_count, head_count, HEAD_SIZE)
    frequency = rope_base ** (-jnp.arange(half_size, dtype=jnp.float32) / half_size)
    angles = positions.astype(jnp.float32)[:, None] * frequency[None, :]
    cosine = jnp.cos(angles)[:, None, :]
    sine_part = jnp.sin(angles)[:, None, :]
    leading = reshaped_rows[..., :half_size]
    second = reshaped_rows[..., half_size:]
    turned = jnp.concatenate(
        [leading * cosine - second * sine_part, second * cosine + leading * sine_part], axis=-1
    )
    return turned.reshape(row_count, head_count * HEAD_SIZE)


def ancestry(parents):
    node_count = parents.shape[-1]
    node_index = jnp.arange(node_count, dtype=jnp.int32)
    parent_step = (parents[..., :, None] == node_index[None, None, :]).astype(jnp.float32)
    closure = jnp.maximum(parent_step, jnp.eye(node_count, dtype=jnp.float32)[None])
    for squaring in range(max(1, (node_count - 1).bit_length())):
        closure = jnp.minimum(jnp.einsum("rij,rjk->rik", closure, closure), 1.0)
    tree_depth = jnp.sum(closure, axis=-1).astype(jnp.int32) - 1
    return (closure, tree_depth)


def attend(query_rows, tree_key_value, cached_row_block, length, closure):
    tree_drafts = query_rows.shape[0]
    queries_per_group = QUERY_HEADS // KEY_VALUE_HEADS
    key_value_width = KEY_VALUE_HEADS * HEAD_SIZE
    reshaped_rows = query_rows.reshape(tree_drafts, KEY_VALUE_HEADS, queries_per_group, HEAD_SIZE)
    cached_key_rows = cached_row_block[:, :key_value_width].reshape(-1, KEY_VALUE_HEADS, HEAD_SIZE)
    cached_value_rows = cached_row_block[:, key_value_width:].reshape(
        -1, KEY_VALUE_HEADS, HEAD_SIZE
    )
    tree_key_rows = tree_key_value[:, :key_value_width].reshape(-1, KEY_VALUE_HEADS, HEAD_SIZE)
    tree_value_rows = tree_key_value[:, key_value_width:].reshape(-1, KEY_VALUE_HEADS, HEAD_SIZE)
    scale = 1.0 / math.sqrt(HEAD_SIZE)
    cache_scores = (
        jnp.einsum(
            "igsd,jgd->gsij", reshaped_rows, cached_key_rows, preferred_element_type=jnp.float32
        )
        * scale
    )
    draft_scores = (
        jnp.einsum(
            "igsd,jgd->gsij", reshaped_rows, tree_key_rows, preferred_element_type=jnp.float32
        )
        * scale
    )
    live_cache = (jnp.arange(cached_row_block.shape[0]) < length)[None, None, None, :]
    live_draft = (closure > 0.5)[None, None, :, :]
    cache_scores = jnp.where(live_cache, cache_scores, -1e30)
    draft_scores = jnp.where(live_draft, draft_scores, -1e30)
    highest = jnp.maximum(jnp.max(cache_scores, axis=-1), jnp.max(draft_scores, axis=-1))[..., None]
    cache_weight = jnp.exp(cache_scores - highest)
    draft_weight = jnp.exp(draft_scores - highest)
    running = jnp.sum(cache_weight, axis=-1, keepdims=True) + jnp.sum(
        draft_weight, axis=-1, keepdims=True
    )
    cache_probs = (cache_weight / running).astype(jnp.bfloat16)
    draft_probs = (draft_weight / running).astype(jnp.bfloat16)
    context = jnp.einsum(
        "gsij,jgd->igsd", cache_probs, cached_value_rows, preferred_element_type=jnp.float32
    )
    context = context + jnp.einsum(
        "gsij,jgd->igsd", draft_probs, tree_value_rows, preferred_element_type=jnp.float32
    )
    return context.reshape(tree_drafts, QUERY_HEADS * HEAD_SIZE).astype(jnp.bfloat16)


def compact(kv_rows, closure, tree_depth, accepted):
    path_mask = jnp.take_along_axis(closure, accepted[:, None, None], axis=1)[:, 0, :]
    level = jnp.arange(kv_rows.shape[1], dtype=jnp.int32)
    select = (
        path_mask[:, None, :] * (tree_depth[:, None, :] == level[None, :, None]).astype(jnp.float32)
    ).astype(jnp.bfloat16)
    return jnp.einsum("rtj,rjw->rtw", select, kv_rows, preferred_element_type=jnp.float32).astype(
        jnp.bfloat16
    )


def slot_tables(routes, capacity):
    rows = routes.shape[0]
    expert_ids = jnp.arange(EXPERTS, dtype=jnp.int32)
    picks = routes[:, :, None] == expert_ids[None, None, :]
    chosen = jnp.sum(picks.astype(jnp.int32), axis=1).astype(jnp.bfloat16)
    row_ids = jnp.arange(rows, dtype=jnp.int32)
    before = (row_ids[None, :] < row_ids[:, None]).astype(jnp.bfloat16)
    earlier = jnp.dot(before, chosen, preferred_element_type=jnp.float32).astype(jnp.int32)
    slot_number = jnp.sum(jnp.where(picks, earlier[:, None, :], 0), axis=2)
    slot_index = routes * capacity + slot_number
    slot_ids = jnp.arange(EXPERTS * capacity, dtype=jnp.int32)
    hit = slot_index[:, :, None] == slot_ids[None, None, :]
    return hit


def pack_slots(token_rows, hit):
    place = jnp.sum(hit.astype(jnp.bfloat16), axis=1)
    return jnp.einsum("ts,td->sd", place, token_rows, preferred_element_type=jnp.bfloat16)


def expert_products(received, w_gate, w_up, w_down):
    gate_part = jnp.einsum("pekd,edf->pekf", received, w_gate, preferred_element_type=jnp.float32)
    up_part = jnp.einsum("pekd,edf->pekf", received, w_up, preferred_element_type=jnp.float32)
    hidden = (jnp.maximum(gate_part, 0.0) * up_part).astype(jnp.bfloat16)
    return jnp.einsum("pekf,efd->pekd", hidden, w_down, preferred_element_type=jnp.float32).astype(
        jnp.bfloat16
    )


def combine_picks(returned_rows, hit, gate_weights):
    layer_width = returned_rows.shape[-1]
    flat_rows = returned_rows.reshape(-1, layer_width)
    weight = jnp.sum(jnp.where(hit, gate_weights[:, :, None], 0.0), axis=1)
    weight_hi = weight.astype(jnp.bfloat16)
    weight_lo = (weight - weight_hi.astype(jnp.float32)).astype(jnp.bfloat16)
    mixed = jnp.dot(weight_hi, flat_rows, preferred_element_type=jnp.float32)
    return mixed + jnp.dot(weight_lo, flat_rows, preferred_element_type=jnp.float32)


def routed_whole(moe_in, routes, gate_weights, w_gate, w_up, w_down):
    capacity = 2 * CAP
    hit = slot_tables(routes, capacity)
    buffer = pack_slots(moe_in, hit)
    peer_count = lax.axis_size("exp")
    reshaped_rows = buffer.reshape(peer_count, w_gate.shape[0], capacity, moe_in.shape[1])
    produced = expert_products(
        lax.all_to_all(reshaped_rows, "exp", split_axis=0, concat_axis=0, tiled=True),
        w_gate,
        w_up,
        w_down,
    )
    returned_rows = lax.all_to_all(produced, "exp", split_axis=0, concat_axis=0, tiled=True)
    return combine_picks(returned_rows, hit, gate_weights)


def local(
    tokens,
    attn_gain,
    w_query,
    key_projection,
    value_projection,
    w_out,
    moe_gain,
    w_gate,
    w_up,
    w_down,
    routes,
    gate_weights,
    kv_cache,
    lengths,
    parents,
    accepted,
):
    rows_here = tokens.shape[0]
    local_reqs = kv_cache.shape[0]
    normed = rms_scale(tokens, attn_gain)
    closure, tree_depth = ancestry(parents)
    positions = (lengths[:, None] + tree_depth).reshape(-1)
    query_sum = jnp.dot(
        normed,
        lax.all_gather(w_query, "req", axis=0, tiled=True),
        preferred_element_type=jnp.float32,
    )
    key_sum = jnp.dot(
        normed,
        lax.all_gather(key_projection, "req", axis=0, tiled=True),
        preferred_element_type=jnp.float32,
    )
    value_sum = jnp.dot(
        normed,
        lax.all_gather(value_projection, "req", axis=0, tiled=True),
        preferred_element_type=jnp.float32,
    )
    query_rows = rotate(query_sum, positions).astype(jnp.bfloat16)
    tree_key_value = jnp.concatenate([rotate(key_sum, positions), value_sum], axis=1).astype(
        jnp.bfloat16
    )
    query_req = query_rows.reshape(local_reqs, DRAFT_TOKENS, query_rows.shape[1])
    key_value_request = tree_key_value.reshape(local_reqs, DRAFT_TOKENS, tree_key_value.shape[1])
    context = jax.vmap(attend)(query_req, key_value_request, kv_cache, lengths, closure).reshape(
        rows_here, -1
    )
    attn_out = jnp.dot(
        context,
        lax.all_gather(w_out, "req", axis=1, tiled=True),
        preferred_element_type=jnp.float32,
    )
    residual = (tokens.astype(jnp.float32) + attn_out).astype(jnp.bfloat16)
    moe_in = rms_scale(residual, moe_gain)
    mixed = routed_whole(moe_in, routes, gate_weights, w_gate, w_up, w_down)
    layer_out = (residual.astype(jnp.float32) + mixed).astype(jnp.bfloat16)
    new_entries = compact(key_value_request, closure, tree_depth, accepted)
    return (layer_out, new_entries)


def solution(mesh):
    return jax.shard_map(
        local,
        mesh=mesh,
        in_specs=(
            P(("req", "exp"), None),
            P(),
            P("req", None),
            P("req", None),
            P("req", None),
            P(None, "req"),
            P(),
            P("exp", None, None),
            P("exp", None, None),
            P("exp", None, None),
            P(("req", "exp"), None),
            P(("req", "exp"), None),
            P(("req", "exp"), None, None),
            P(("req", "exp")),
            P(("req", "exp"), None),
            P(("req", "exp")),
        ),
        out_specs=(P(("req", "exp"), None), P(("req", "exp"), None, None)),
        check_vma=False,
    )
```

```python
import math

import jax
import jax.numpy as jnp
from jax import lax
from jax.sharding import PartitionSpec as P

QUERY_HEADS = 12
KEY_VALUE_HEADS = 2
HEAD_SIZE = 128
EXPERTS = 32
TOP = 4
DRAFT_TOKENS = 64
CAP = 24
BLOCK_ROWS = 128


eps_norm = 1e-06
rope_base = 1000000.0


def rms_scale(token_rows, gain_vec):
    widened = token_rows.astype(jnp.float32)
    inverse = lax.rsqrt(jnp.mean(widened * widened, axis=-1, keepdims=True) + eps_norm)
    return (widened * inverse * gain_vec).astype(jnp.bfloat16)


def rotate(values, positions):
    row_count = values.shape[0]
    head_count = values.shape[1] // HEAD_SIZE
    half_size = HEAD_SIZE // 2
    reshaped_rows = values.reshape(row_count, head_count, HEAD_SIZE)
    frequency = rope_base ** (-jnp.arange(half_size, dtype=jnp.float32) / half_size)
    angles = positions.astype(jnp.float32)[:, None] * frequency[None, :]
    cosine = jnp.cos(angles)[:, None, :]
    sine_part = jnp.sin(angles)[:, None, :]
    leading = reshaped_rows[..., :half_size]
    second = reshaped_rows[..., half_size:]
    turned = jnp.concatenate(
        [leading * cosine - second * sine_part, second * cosine + leading * sine_part], axis=-1
    )
    return turned.reshape(row_count, head_count * HEAD_SIZE)


def ancestry(parents):
    node_count = parents.shape[-1]
    node_index = jnp.arange(node_count, dtype=jnp.int32)
    parent_step = (parents[..., :, None] == node_index[None, None, :]).astype(jnp.float32)
    closure = jnp.maximum(parent_step, jnp.eye(node_count, dtype=jnp.float32)[None])
    for squaring in range(max(1, (node_count - 1).bit_length())):
        closure = jnp.minimum(jnp.einsum("rij,rjk->rik", closure, closure), 1.0)
    tree_depth = jnp.sum(closure, axis=-1).astype(jnp.int32) - 1
    return (closure, tree_depth)


def attend(query_rows, tree_key_value, cached_row_block, length, closure):
    tree_drafts = query_rows.shape[0]
    queries_per_group = QUERY_HEADS // KEY_VALUE_HEADS
    key_value_width = KEY_VALUE_HEADS * HEAD_SIZE
    reshaped_rows = query_rows.reshape(tree_drafts, KEY_VALUE_HEADS, queries_per_group, HEAD_SIZE)
    cached_key_rows = cached_row_block[:, :key_value_width].reshape(-1, KEY_VALUE_HEADS, HEAD_SIZE)
    cached_value_rows = cached_row_block[:, key_value_width:].reshape(
        -1, KEY_VALUE_HEADS, HEAD_SIZE
    )
    tree_key_rows = tree_key_value[:, :key_value_width].reshape(-1, KEY_VALUE_HEADS, HEAD_SIZE)
    tree_value_rows = tree_key_value[:, key_value_width:].reshape(-1, KEY_VALUE_HEADS, HEAD_SIZE)
    scale = 1.0 / math.sqrt(HEAD_SIZE)
    cache_scores = (
        jnp.einsum(
            "igsd,jgd->gsij", reshaped_rows, cached_key_rows, preferred_element_type=jnp.float32
        )
        * scale
    )
    draft_scores = (
        jnp.einsum(
            "igsd,jgd->gsij", reshaped_rows, tree_key_rows, preferred_element_type=jnp.float32
        )
        * scale
    )
    live_cache = (jnp.arange(cached_row_block.shape[0]) < length)[None, None, None, :]
    live_draft = (closure > 0.5)[None, None, :, :]
    cache_scores = jnp.where(live_cache, cache_scores, -1e30)
    draft_scores = jnp.where(live_draft, draft_scores, -1e30)
    highest = jnp.maximum(jnp.max(cache_scores, axis=-1), jnp.max(draft_scores, axis=-1))[..., None]
    cache_weight = jnp.exp(cache_scores - highest)
    draft_weight = jnp.exp(draft_scores - highest)
    running = jnp.sum(cache_weight, axis=-1, keepdims=True) + jnp.sum(
        draft_weight, axis=-1, keepdims=True
    )
    cache_probs = (cache_weight / running).astype(jnp.bfloat16)
    draft_probs = (draft_weight / running).astype(jnp.bfloat16)
    context = jnp.einsum(
        "gsij,jgd->igsd", cache_probs, cached_value_rows, preferred_element_type=jnp.float32
    )
    context = context + jnp.einsum(
        "gsij,jgd->igsd", draft_probs, tree_value_rows, preferred_element_type=jnp.float32
    )
    return context.reshape(tree_drafts, QUERY_HEADS * HEAD_SIZE).astype(jnp.bfloat16)


def compact(kv_rows, closure, tree_depth, accepted):
    path_mask = jnp.take_along_axis(closure, accepted[:, None, None], axis=1)[:, 0, :]
    level = jnp.arange(kv_rows.shape[1], dtype=jnp.int32)
    select = (
        path_mask[:, None, :] * (tree_depth[:, None, :] == level[None, :, None]).astype(jnp.float32)
    ).astype(jnp.bfloat16)
    return jnp.einsum("rtj,rjw->rtw", select, kv_rows, preferred_element_type=jnp.float32).astype(
        jnp.bfloat16
    )


def slot_tables(routes, capacity):
    rows = routes.shape[0]
    expert_ids = jnp.arange(EXPERTS, dtype=jnp.int32)
    picks = routes[:, :, None] == expert_ids[None, None, :]
    chosen = jnp.sum(picks.astype(jnp.int32), axis=1).astype(jnp.bfloat16)
    row_ids = jnp.arange(rows, dtype=jnp.int32)
    before = (row_ids[None, :] < row_ids[:, None]).astype(jnp.bfloat16)
    earlier = jnp.dot(before, chosen, preferred_element_type=jnp.float32).astype(jnp.int32)
    slot_number = jnp.sum(jnp.where(picks, earlier[:, None, :], 0), axis=2)
    slot_index = routes * capacity + slot_number
    slot_ids = jnp.arange(EXPERTS * capacity, dtype=jnp.int32)
    hit = slot_index[:, :, None] == slot_ids[None, None, :]
    return hit


def pack_slots(token_rows, hit):
    place = jnp.sum(hit.astype(jnp.bfloat16), axis=1)
    return jnp.einsum("ts,td->sd", place, token_rows, preferred_element_type=jnp.bfloat16)


def expert_products(received, w_gate, w_up, w_down):
    gate_part = jnp.einsum("pekd,edf->pekf", received, w_gate, preferred_element_type=jnp.float32)
    up_part = jnp.einsum("pekd,edf->pekf", received, w_up, preferred_element_type=jnp.float32)
    hidden = (jnp.maximum(gate_part, 0.0) * up_part).astype(jnp.bfloat16)
    return jnp.einsum("pekf,efd->pekd", hidden, w_down, preferred_element_type=jnp.float32).astype(
        jnp.bfloat16
    )


def combine_picks(returned_rows, hit, gate_weights):
    layer_width = returned_rows.shape[-1]
    flat_rows = returned_rows.reshape(-1, layer_width)
    weight = jnp.sum(jnp.where(hit, gate_weights[:, :, None], 0.0), axis=1)
    weight_hi = weight.astype(jnp.bfloat16)
    weight_lo = (weight - weight_hi.astype(jnp.float32)).astype(jnp.bfloat16)
    mixed = jnp.dot(weight_hi, flat_rows, preferred_element_type=jnp.float32)
    return mixed + jnp.dot(weight_lo, flat_rows, preferred_element_type=jnp.float32)


def routed_whole(moe_in, routes, gate_weights, w_gate, w_up, w_down):
    capacity = CAP * (moe_in.shape[0] // BLOCK_ROWS)
    hit = slot_tables(routes, capacity)
    buffer = pack_slots(moe_in, hit)
    peer_count = lax.axis_size("exp")
    reshaped_rows = buffer.reshape(peer_count, w_gate.shape[0], capacity, moe_in.shape[1])
    produced = expert_products(
        lax.all_to_all(reshaped_rows, "exp", split_axis=0, concat_axis=0, tiled=True),
        w_gate,
        w_up,
        w_down,
    )
    returned_rows = lax.all_to_all(produced, "exp", split_axis=0, concat_axis=0, tiled=True)
    return combine_picks(returned_rows, hit, gate_weights)


def local(
    tokens,
    attn_gain,
    w_query,
    key_projection,
    value_projection,
    w_out,
    moe_gain,
    w_gate,
    w_up,
    w_down,
    routes,
    gate_weights,
    kv_cache,
    lengths,
    parents,
    accepted,
):
    rows_here = tokens.shape[0]
    local_reqs = kv_cache.shape[0]
    normed = rms_scale(tokens, attn_gain)
    closure, tree_depth = ancestry(parents)
    positions = (lengths[:, None] + tree_depth).reshape(-1)
    query_sum = jnp.dot(
        normed,
        lax.all_gather(w_query, "req", axis=0, tiled=True),
        preferred_element_type=jnp.float32,
    )
    key_sum = jnp.dot(
        normed,
        lax.all_gather(key_projection, "req", axis=0, tiled=True),
        preferred_element_type=jnp.float32,
    )
    value_sum = jnp.dot(
        normed,
        lax.all_gather(value_projection, "req", axis=0, tiled=True),
        preferred_element_type=jnp.float32,
    )
    query_rows = rotate(query_sum, positions).astype(jnp.bfloat16)
    tree_key_value = jnp.concatenate([rotate(key_sum, positions), value_sum], axis=1).astype(
        jnp.bfloat16
    )
    query_req = query_rows.reshape(local_reqs, DRAFT_TOKENS, query_rows.shape[1])
    key_value_request = tree_key_value.reshape(local_reqs, DRAFT_TOKENS, tree_key_value.shape[1])
    w_out_full = lax.all_gather(w_out, "req", axis=1, tiled=True)
    chunk_count = rows_here // BLOCK_ROWS
    reqs_per_chunk = local_reqs // chunk_count
    outs = []
    for chunk in range(chunk_count):
        rq = slice(chunk * reqs_per_chunk, (chunk + 1) * reqs_per_chunk)
        rw = slice(chunk * BLOCK_ROWS, (chunk + 1) * BLOCK_ROWS)
        context = jax.vmap(attend)(
            query_req[rq], key_value_request[rq], kv_cache[rq], lengths[rq], closure[rq]
        ).reshape(BLOCK_ROWS, -1)
        attn_out = jnp.dot(context, w_out_full, preferred_element_type=jnp.float32)
        residual = (tokens[rw].astype(jnp.float32) + attn_out).astype(jnp.bfloat16)
        moe_in = rms_scale(residual, moe_gain)
        mixed = routed_whole(moe_in, routes[rw], gate_weights[rw], w_gate, w_up, w_down)
        outs.append((residual.astype(jnp.float32) + mixed).astype(jnp.bfloat16))
    layer_out = jnp.concatenate(outs, axis=0)
    new_entries = compact(key_value_request, closure, tree_depth, accepted)
    return (layer_out, new_entries)


def solution(mesh):
    return jax.shard_map(
        local,
        mesh=mesh,
        in_specs=(
            P(("req", "exp"), None),
            P(),
            P("req", None),
            P("req", None),
            P("req", None),
            P(None, "req"),
            P(),
            P("exp", None, None),
            P("exp", None, None),
            P("exp", None, None),
            P(("req", "exp"), None),
            P(("req", "exp"), None),
            P(("req", "exp"), None, None),
            P(("req", "exp")),
            P(("req", "exp"), None),
            P(("req", "exp")),
        ),
        out_specs=(P(("req", "exp"), None), P(("req", "exp"), None, None)),
        check_vma=False,
    )
```

```python
import functools
import math

import jax
import jax.numpy as jnp
from jax import lax
from jax.sharding import PartitionSpec as P

QUERY_HEADS = 12
KEY_VALUE_HEADS = 2
HEAD_SIZE = 128
EXPERTS = 32
TOP = 4
DRAFT_TOKENS = 64
CAP = 24
BLOCK_ROWS = 128


eps_norm = 1e-06
rope_base = 1000000.0


def rms_scale(token_rows, gain_vec):
    widened = token_rows.astype(jnp.float32)
    inverse = lax.rsqrt(jnp.mean(widened * widened, axis=-1, keepdims=True) + eps_norm)
    return (widened * inverse * gain_vec).astype(jnp.bfloat16)


def rotate(values, positions):
    row_count = values.shape[0]
    head_count = values.shape[1] // HEAD_SIZE
    half_size = HEAD_SIZE // 2
    reshaped_rows = values.reshape(row_count, head_count, HEAD_SIZE)
    frequency = rope_base ** (-jnp.arange(half_size, dtype=jnp.float32) / half_size)
    angles = positions.astype(jnp.float32)[:, None] * frequency[None, :]
    cosine = jnp.cos(angles)[:, None, :]
    sine_part = jnp.sin(angles)[:, None, :]
    leading = reshaped_rows[..., :half_size]
    second = reshaped_rows[..., half_size:]
    turned = jnp.concatenate(
        [leading * cosine - second * sine_part, second * cosine + leading * sine_part], axis=-1
    )
    return turned.reshape(row_count, head_count * HEAD_SIZE)


def ancestry(parents):
    node_count = parents.shape[-1]
    node_index = jnp.arange(node_count, dtype=jnp.int32)
    parent_step = (parents[..., :, None] == node_index[None, None, :]).astype(jnp.float32)
    closure = jnp.maximum(parent_step, jnp.eye(node_count, dtype=jnp.float32)[None])
    for squaring in range(max(1, (node_count - 1).bit_length())):
        closure = jnp.minimum(jnp.einsum("rij,rjk->rik", closure, closure), 1.0)
    tree_depth = jnp.sum(closure, axis=-1).astype(jnp.int32) - 1
    return (closure, tree_depth)


def attend(query_rows, tree_key_value, cached_row_block, length, closure):
    tree_drafts = query_rows.shape[0]
    queries_per_group = QUERY_HEADS // KEY_VALUE_HEADS
    key_value_width = KEY_VALUE_HEADS * HEAD_SIZE
    reshaped_rows = query_rows.reshape(tree_drafts, KEY_VALUE_HEADS, queries_per_group, HEAD_SIZE)
    cached_key_rows = cached_row_block[:, :key_value_width].reshape(-1, KEY_VALUE_HEADS, HEAD_SIZE)
    cached_value_rows = cached_row_block[:, key_value_width:].reshape(
        -1, KEY_VALUE_HEADS, HEAD_SIZE
    )
    tree_key_rows = tree_key_value[:, :key_value_width].reshape(-1, KEY_VALUE_HEADS, HEAD_SIZE)
    tree_value_rows = tree_key_value[:, key_value_width:].reshape(-1, KEY_VALUE_HEADS, HEAD_SIZE)
    scale = 1.0 / math.sqrt(HEAD_SIZE)
    cache_scores = (
        jnp.einsum(
            "igsd,jgd->gsij", reshaped_rows, cached_key_rows, preferred_element_type=jnp.float32
        )
        * scale
    )
    draft_scores = (
        jnp.einsum(
            "igsd,jgd->gsij", reshaped_rows, tree_key_rows, preferred_element_type=jnp.float32
        )
        * scale
    )
    live_cache = (jnp.arange(cached_row_block.shape[0]) < length)[None, None, None, :]
    live_draft = (closure > 0.5)[None, None, :, :]
    cache_scores = jnp.where(live_cache, cache_scores, -1e30)
    draft_scores = jnp.where(live_draft, draft_scores, -1e30)
    highest = jnp.maximum(jnp.max(cache_scores, axis=-1), jnp.max(draft_scores, axis=-1))[..., None]
    cache_weight = jnp.exp(cache_scores - highest)
    draft_weight = jnp.exp(draft_scores - highest)
    running = jnp.sum(cache_weight, axis=-1, keepdims=True) + jnp.sum(
        draft_weight, axis=-1, keepdims=True
    )
    cache_probs = (cache_weight / running).astype(jnp.bfloat16)
    draft_probs = (draft_weight / running).astype(jnp.bfloat16)
    context = jnp.einsum(
        "gsij,jgd->igsd", cache_probs, cached_value_rows, preferred_element_type=jnp.float32
    )
    context = context + jnp.einsum(
        "gsij,jgd->igsd", draft_probs, tree_value_rows, preferred_element_type=jnp.float32
    )
    return context.reshape(tree_drafts, QUERY_HEADS * HEAD_SIZE).astype(jnp.bfloat16)


def compact(kv_rows, closure, tree_depth, accepted):
    path_mask = jnp.take_along_axis(closure, accepted[:, None, None], axis=1)[:, 0, :]
    level = jnp.arange(kv_rows.shape[1], dtype=jnp.int32)
    select = (
        path_mask[:, None, :] * (tree_depth[:, None, :] == level[None, :, None]).astype(jnp.float32)
    ).astype(jnp.bfloat16)
    return jnp.einsum("rtj,rjw->rtw", select, kv_rows, preferred_element_type=jnp.float32).astype(
        jnp.bfloat16
    )


def slot_tables(routes, capacity, local_experts, grid):
    rows = routes.shape[0]
    ny = grid[1]
    me = lax.axis_index("exp")
    owner = routes // local_experts
    dx = (owner // ny - me // ny) % grid[0]
    dy = (owner % ny - me % ny) % ny
    block = (dx * ny + dy) * local_experts + routes % local_experts
    expert_ids = jnp.arange(EXPERTS, dtype=jnp.int32)
    picks = routes[:, :, None] == expert_ids[None, None, :]
    chosen = jnp.sum(picks.astype(jnp.int32), axis=1).astype(jnp.bfloat16)
    row_ids = jnp.arange(rows, dtype=jnp.int32)
    before = (row_ids[None, :] < row_ids[:, None]).astype(jnp.bfloat16)
    earlier = jnp.dot(before, chosen, preferred_element_type=jnp.float32).astype(jnp.int32)
    slot_number = jnp.sum(jnp.where(picks, earlier[:, None, :], 0), axis=2)
    slot_index = block * capacity + slot_number
    slot_ids = jnp.arange(EXPERTS * capacity, dtype=jnp.int32)
    hit = slot_index[:, :, None] == slot_ids[None, None, :]
    return hit


def pack_slots(token_rows, hit):
    place = jnp.sum(hit.astype(jnp.bfloat16), axis=1)
    return jnp.einsum("ts,td->sd", place, token_rows, preferred_element_type=jnp.bfloat16)


def expert_products(received, w_gate, w_up, w_down):
    gate_part = jnp.einsum("esd,edf->esf", received, w_gate, preferred_element_type=jnp.float32)
    up_part = jnp.einsum("esd,edf->esf", received, w_up, preferred_element_type=jnp.float32)
    hidden = (jnp.maximum(gate_part, 0.0) * up_part).astype(jnp.bfloat16)
    return jnp.einsum("esf,efd->esd", hidden, w_down, preferred_element_type=jnp.float32).astype(
        jnp.bfloat16
    )


def shift_pairs(offset, grid, inverse):
    nx, ny = grid
    dx, dy = offset // ny, offset % ny
    pairs = []
    for src_x in range(nx):
        for src_y in range(ny):
            dst = ((src_x + dx) % nx) * ny + (src_y + dy) % ny
            pairs.append((dst, src_x * ny + src_y) if inverse else (src_x * ny + src_y, dst))
    return pairs


def combine_picks(returned_rows, hit, gate_weights):
    layer_width = returned_rows.shape[-1]
    flat_rows = returned_rows.reshape(-1, layer_width)
    weight = jnp.sum(jnp.where(hit, gate_weights[:, :, None], 0.0), axis=1)
    weight_hi = weight.astype(jnp.bfloat16)
    weight_lo = (weight - weight_hi.astype(jnp.float32)).astype(jnp.bfloat16)
    mixed = jnp.dot(weight_hi, flat_rows, preferred_element_type=jnp.float32)
    return mixed + jnp.dot(weight_lo, flat_rows, preferred_element_type=jnp.float32)


def routed_whole(moe_in, routes, gate_weights, w_gate, w_up, w_down, grid):
    capacity = CAP * (moe_in.shape[0] // BLOCK_ROWS)
    local_experts = w_gate.shape[0]
    peer_count = grid[0] * grid[1]
    width = moe_in.shape[1]
    hit = slot_tables(routes, capacity, local_experts, grid)
    buffer = pack_slots(moe_in, hit).reshape(peer_count, local_experts, capacity, width)
    arrived = [buffer[0]] + [
        lax.ppermute(buffer[r], "exp", shift_pairs(r, grid, False)) for r in range(1, peer_count)
    ]
    received = jnp.stack(arrived, axis=1).reshape(local_experts, peer_count * capacity, width)
    produced = expert_products(received, w_gate, w_up, w_down).reshape(
        local_experts, peer_count, capacity, width
    )
    returned = [produced[:, 0]] + [
        lax.ppermute(produced[:, r], "exp", shift_pairs(r, grid, True))
        for r in range(1, peer_count)
    ]
    returned_rows = jnp.stack(returned, axis=0)
    return combine_picks(returned_rows, hit, gate_weights)


def local(
    grid,
    tokens,
    attn_gain,
    w_query,
    key_projection,
    value_projection,
    w_out,
    moe_gain,
    w_gate,
    w_up,
    w_down,
    routes,
    gate_weights,
    kv_cache,
    lengths,
    parents,
    accepted,
):
    rows_here = tokens.shape[0]
    local_reqs = kv_cache.shape[0]
    normed = rms_scale(tokens, attn_gain)
    closure, tree_depth = ancestry(parents)
    positions = (lengths[:, None] + tree_depth).reshape(-1)
    query_sum = jnp.dot(
        normed,
        lax.all_gather(w_query, "req", axis=0, tiled=True),
        preferred_element_type=jnp.float32,
    )
    key_sum = jnp.dot(
        normed,
        lax.all_gather(key_projection, "req", axis=0, tiled=True),
        preferred_element_type=jnp.float32,
    )
    value_sum = jnp.dot(
        normed,
        lax.all_gather(value_projection, "req", axis=0, tiled=True),
        preferred_element_type=jnp.float32,
    )
    query_rows = rotate(query_sum, positions).astype(jnp.bfloat16)
    tree_key_value = jnp.concatenate([rotate(key_sum, positions), value_sum], axis=1).astype(
        jnp.bfloat16
    )
    query_req = query_rows.reshape(local_reqs, DRAFT_TOKENS, query_rows.shape[1])
    key_value_request = tree_key_value.reshape(local_reqs, DRAFT_TOKENS, tree_key_value.shape[1])
    w_out_full = lax.all_gather(w_out, "req", axis=1, tiled=True)
    chunk_count = rows_here // BLOCK_ROWS
    reqs_per_chunk = local_reqs // chunk_count
    outs = []
    for chunk in range(chunk_count):
        rq = slice(chunk * reqs_per_chunk, (chunk + 1) * reqs_per_chunk)
        rw = slice(chunk * BLOCK_ROWS, (chunk + 1) * BLOCK_ROWS)
        context = jax.vmap(attend)(
            query_req[rq], key_value_request[rq], kv_cache[rq], lengths[rq], closure[rq]
        ).reshape(BLOCK_ROWS, -1)
        attn_out = jnp.dot(context, w_out_full, preferred_element_type=jnp.float32)
        residual = (tokens[rw].astype(jnp.float32) + attn_out).astype(jnp.bfloat16)
        moe_in = rms_scale(residual, moe_gain)
        mixed = routed_whole(
            moe_in, routes[rw], gate_weights[rw], w_gate, w_up, w_down, grid
        )
        outs.append((residual.astype(jnp.float32) + mixed).astype(jnp.bfloat16))
    layer_out = jnp.concatenate(outs, axis=0)
    new_entries = compact(key_value_request, closure, tree_depth, accepted)
    return (layer_out, new_entries)


def exp_grid(mesh):
    row = mesh.devices[0]
    ny = len({tuple(d.coords)[1] for d in row})
    return (row.size // ny, ny)


def solution(mesh):
    return jax.shard_map(
        functools.partial(local, exp_grid(mesh)),
        mesh=mesh,
        in_specs=(
            P(("req", "exp"), None),
            P(),
            P("req", None),
            P("req", None),
            P("req", None),
            P(None, "req"),
            P(),
            P("exp", None, None),
            P("exp", None, None),
            P("exp", None, None),
            P(("req", "exp"), None),
            P(("req", "exp"), None),
            P(("req", "exp"), None, None),
            P(("req", "exp")),
            P(("req", "exp"), None),
            P(("req", "exp")),
        ),
        out_specs=(P(("req", "exp"), None), P(("req", "exp"), None, None)),
        check_vma=False,
    )
```

```python
import math

import jax
import jax.numpy as jnp
from jax import lax
from jax.sharding import PartitionSpec as P

QUERY_HEADS = 12
KEY_VALUE_HEADS = 2
HEAD_SIZE = 128
EXPERTS = 32
TOP = 4
DRAFT_TOKENS = 64
CAP = 24
BLOCK_ROWS = 128


eps_norm = 1e-06
rope_base = 1000000.0


def rms_scale(token_rows, gain_vec):
    widened = token_rows.astype(jnp.float32)
    inverse = lax.rsqrt(jnp.mean(widened * widened, axis=-1, keepdims=True) + eps_norm)
    return (widened * inverse * gain_vec).astype(jnp.bfloat16)


def rotate(values, positions):
    row_count = values.shape[0]
    head_count = values.shape[1] // HEAD_SIZE
    half_size = HEAD_SIZE // 2
    reshaped_rows = values.reshape(row_count, head_count, HEAD_SIZE)
    frequency = rope_base ** (-jnp.arange(half_size, dtype=jnp.float32) / half_size)
    angles = positions.astype(jnp.float32)[:, None] * frequency[None, :]
    cosine = jnp.cos(angles)[:, None, :]
    sine_part = jnp.sin(angles)[:, None, :]
    leading = reshaped_rows[..., :half_size]
    second = reshaped_rows[..., half_size:]
    turned = jnp.concatenate(
        [leading * cosine - second * sine_part, second * cosine + leading * sine_part], axis=-1
    )
    return turned.reshape(row_count, head_count * HEAD_SIZE)


def ancestry(parents):
    node_count = parents.shape[-1]
    node_index = jnp.arange(node_count, dtype=jnp.int32)
    parent_step = (parents[..., :, None] == node_index[None, None, :]).astype(jnp.float32)
    closure = jnp.maximum(parent_step, jnp.eye(node_count, dtype=jnp.float32)[None])
    for squaring in range(max(1, (node_count - 1).bit_length())):
        closure = jnp.minimum(jnp.einsum("rij,rjk->rik", closure, closure), 1.0)
    tree_depth = jnp.sum(closure, axis=-1).astype(jnp.int32) - 1
    return (closure, tree_depth)


def attend(query_rows, tree_key_value, cached_row_block, length, closure):
    tree_drafts = query_rows.shape[0]
    queries_per_group = QUERY_HEADS // KEY_VALUE_HEADS
    key_value_width = KEY_VALUE_HEADS * HEAD_SIZE
    reshaped_rows = query_rows.reshape(tree_drafts, KEY_VALUE_HEADS, queries_per_group, HEAD_SIZE)
    cached_key_rows = cached_row_block[:, :key_value_width].reshape(-1, KEY_VALUE_HEADS, HEAD_SIZE)
    cached_value_rows = cached_row_block[:, key_value_width:].reshape(
        -1, KEY_VALUE_HEADS, HEAD_SIZE
    )
    tree_key_rows = tree_key_value[:, :key_value_width].reshape(-1, KEY_VALUE_HEADS, HEAD_SIZE)
    tree_value_rows = tree_key_value[:, key_value_width:].reshape(-1, KEY_VALUE_HEADS, HEAD_SIZE)
    scale = 1.0 / math.sqrt(HEAD_SIZE)
    cache_scores = (
        jnp.einsum(
            "igsd,jgd->gsij", reshaped_rows, cached_key_rows, preferred_element_type=jnp.float32
        )
        * scale
    )
    draft_scores = (
        jnp.einsum(
            "igsd,jgd->gsij", reshaped_rows, tree_key_rows, preferred_element_type=jnp.float32
        )
        * scale
    )
    live_cache = (jnp.arange(cached_row_block.shape[0]) < length)[None, None, None, :]
    live_draft = (closure > 0.5)[None, None, :, :]
    cache_scores = jnp.where(live_cache, cache_scores, -1e30)
    draft_scores = jnp.where(live_draft, draft_scores, -1e30)
    highest = jnp.maximum(jnp.max(cache_scores, axis=-1), jnp.max(draft_scores, axis=-1))[..., None]
    cache_weight = jnp.exp(cache_scores - highest)
    draft_weight = jnp.exp(draft_scores - highest)
    running = jnp.sum(cache_weight, axis=-1, keepdims=True) + jnp.sum(
        draft_weight, axis=-1, keepdims=True
    )
    cache_probs = (cache_weight / running).astype(jnp.bfloat16)
    draft_probs = (draft_weight / running).astype(jnp.bfloat16)
    context = jnp.einsum(
        "gsij,jgd->igsd", cache_probs, cached_value_rows, preferred_element_type=jnp.float32
    )
    context = context + jnp.einsum(
        "gsij,jgd->igsd", draft_probs, tree_value_rows, preferred_element_type=jnp.float32
    )
    return context.reshape(tree_drafts, QUERY_HEADS * HEAD_SIZE).astype(jnp.bfloat16)


def compact(kv_rows, closure, tree_depth, accepted):
    path_mask = jnp.take_along_axis(closure, accepted[:, None, None], axis=1)[:, 0, :]
    level = jnp.arange(kv_rows.shape[1], dtype=jnp.int32)
    select = (
        path_mask[:, None, :] * (tree_depth[:, None, :] == level[None, :, None]).astype(jnp.float32)
    ).astype(jnp.bfloat16)
    return jnp.einsum("rtj,rjw->rtw", select, kv_rows, preferred_element_type=jnp.float32).astype(
        jnp.bfloat16
    )


def slot_tables(routes, capacity):
    rows = routes.shape[0]
    expert_ids = jnp.arange(EXPERTS, dtype=jnp.int32)
    picks = routes[:, :, None] == expert_ids[None, None, :]
    chosen = jnp.sum(picks.astype(jnp.int32), axis=1).astype(jnp.bfloat16)
    row_ids = jnp.arange(rows, dtype=jnp.int32)
    before = (row_ids[None, :] < row_ids[:, None]).astype(jnp.bfloat16)
    earlier = jnp.dot(before, chosen, preferred_element_type=jnp.float32).astype(jnp.int32)
    slot_number = jnp.sum(jnp.where(picks, earlier[:, None, :], 0), axis=2)
    slot_index = routes * capacity + slot_number
    slot_ids = jnp.arange(EXPERTS * capacity, dtype=jnp.int32)
    hit = slot_index[:, :, None] == slot_ids[None, None, :]
    return hit


def pack_slots(token_rows, hit):
    place = jnp.sum(hit.astype(jnp.bfloat16), axis=1)
    return jnp.einsum("ts,td->sd", place, token_rows, preferred_element_type=jnp.bfloat16)


def expert_products(received, w_gate, w_up, w_down):
    gate_part = jnp.einsum("pekd,edf->pekf", received, w_gate, preferred_element_type=jnp.float32)
    up_part = jnp.einsum("pekd,edf->pekf", received, w_up, preferred_element_type=jnp.float32)
    hidden = (jnp.maximum(gate_part, 0.0) * up_part).astype(jnp.bfloat16)
    return jnp.einsum("pekf,efd->pekd", hidden, w_down, preferred_element_type=jnp.float32).astype(
        jnp.bfloat16
    )


def combine_picks(returned_rows, hit, gate_weights):
    layer_width = returned_rows.shape[-1]
    flat_rows = returned_rows.reshape(-1, layer_width)
    weight = jnp.sum(jnp.where(hit, gate_weights[:, :, None], 0.0), axis=1)
    weight_hi = weight.astype(jnp.bfloat16)
    weight_lo = (weight - weight_hi.astype(jnp.float32)).astype(jnp.bfloat16)
    mixed = jnp.dot(weight_hi, flat_rows, preferred_element_type=jnp.float32)
    return mixed + jnp.dot(weight_lo, flat_rows, preferred_element_type=jnp.float32)


def routed_whole(moe_in, routes, gate_weights, w_gate, w_up, w_down):
    capacity = CAP * (moe_in.shape[0] // BLOCK_ROWS)
    hit = slot_tables(routes, capacity)
    buffer = pack_slots(moe_in, hit)
    peer_count = lax.axis_size("exp")
    reshaped_rows = buffer.reshape(peer_count, w_gate.shape[0], capacity, moe_in.shape[1])
    produced = expert_products(
        lax.all_to_all(reshaped_rows, "exp", split_axis=0, concat_axis=0, tiled=True),
        w_gate,
        w_up,
        w_down,
    )
    returned_rows = lax.all_to_all(produced, "exp", split_axis=0, concat_axis=0, tiled=True)
    return combine_picks(returned_rows, hit, gate_weights)


def two_stage_gather(shard, axis, plane_count, core_count):
    same_core = [[p * core_count + c for p in range(plane_count)] for c in range(core_count)]
    pairs = [[p * core_count + c for c in range(core_count)] for p in range(plane_count)]
    across = lax.all_gather(shard, "req", axis=axis, tiled=True, axis_index_groups=same_core)
    return lax.all_gather(across, "req", axis=0, tiled=False, axis_index_groups=pairs)


def local(
    tokens,
    attn_gain,
    w_query,
    key_projection,
    value_projection,
    w_out,
    moe_gain,
    w_gate,
    w_up,
    w_down,
    routes,
    gate_weights,
    kv_cache,
    lengths,
    parents,
    accepted,
):
    rows_here = tokens.shape[0]
    local_reqs = kv_cache.shape[0]
    normed = rms_scale(tokens, attn_gain)
    closure, tree_depth = ancestry(parents)
    positions = (lengths[:, None] + tree_depth).reshape(-1)
    core_count = 2
    plane_count = lax.axis_size("req") // core_count
    joined = jnp.concatenate([w_query, key_projection, value_projection], axis=1)
    gathered = two_stage_gather(joined, 0, plane_count, core_count).reshape(-1, joined.shape[1])
    out_cols = w_out.shape[1]
    w_out_after, gathered = lax.optimization_barrier((w_out, gathered))
    shard_rows = w_query.shape[0]
    normed_perm = (
        normed.reshape(rows_here, plane_count, core_count, shard_rows)
        .transpose(0, 2, 1, 3)
        .reshape(rows_here, -1)
    )
    qkv_sum = jnp.dot(normed_perm, gathered, preferred_element_type=jnp.float32)
    query_width = w_query.shape[1]
    kv_width = key_projection.shape[1]
    query_sum = qkv_sum[:, :query_width]
    key_sum = qkv_sum[:, query_width : query_width + kv_width]
    value_sum = qkv_sum[:, query_width + kv_width :]
    query_rows = rotate(query_sum, positions).astype(jnp.bfloat16)
    tree_key_value = jnp.concatenate([rotate(key_sum, positions), value_sum], axis=1).astype(
        jnp.bfloat16
    )
    query_req = query_rows.reshape(local_reqs, DRAFT_TOKENS, query_rows.shape[1])
    key_value_request = tree_key_value.reshape(local_reqs, DRAFT_TOKENS, tree_key_value.shape[1])
    w_out_full = (
        two_stage_gather(w_out_after, 1, plane_count, core_count)
        .transpose(1, 0, 2)
        .reshape(w_out.shape[0], -1)
    )
    chunk_count = rows_here // BLOCK_ROWS
    reqs_per_chunk = local_reqs // chunk_count
    outs = []
    for chunk in range(chunk_count):
        rq = slice(chunk * reqs_per_chunk, (chunk + 1) * reqs_per_chunk)
        rw = slice(chunk * BLOCK_ROWS, (chunk + 1) * BLOCK_ROWS)
        context = jax.vmap(attend)(
            query_req[rq], key_value_request[rq], kv_cache[rq], lengths[rq], closure[rq]
        ).reshape(BLOCK_ROWS, -1)
        attn_out = (
            jnp.dot(context, w_out_full, preferred_element_type=jnp.float32)
            .reshape(BLOCK_ROWS, core_count, plane_count, out_cols)
            .transpose(0, 2, 1, 3)
            .reshape(BLOCK_ROWS, -1)
        )
        residual = (tokens[rw].astype(jnp.float32) + attn_out).astype(jnp.bfloat16)
        moe_in = rms_scale(residual, moe_gain)
        mixed = routed_whole(moe_in, routes[rw], gate_weights[rw], w_gate, w_up, w_down)
        outs.append((residual.astype(jnp.float32) + mixed).astype(jnp.bfloat16))
    layer_out = jnp.concatenate(outs, axis=0)
    new_entries = compact(key_value_request, closure, tree_depth, accepted)
    return (layer_out, new_entries)


def solution(mesh):
    return jax.shard_map(
        local,
        mesh=mesh,
        in_specs=(
            P(("req", "exp"), None),
            P(),
            P("req", None),
            P("req", None),
            P("req", None),
            P(None, "req"),
            P(),
            P("exp", None, None),
            P("exp", None, None),
            P("exp", None, None),
            P(("req", "exp"), None),
            P(("req", "exp"), None),
            P(("req", "exp"), None, None),
            P(("req", "exp")),
            P(("req", "exp"), None),
            P(("req", "exp")),
        ),
        out_specs=(P(("req", "exp"), None), P(("req", "exp"), None, None)),
        check_vma=False,
    )
```

```python
import math

import jax
import jax.numpy as jnp
from jax import lax
from jax.sharding import PartitionSpec as P

QUERY_HEADS = 12
KEY_VALUE_HEADS = 2
HEAD_SIZE = 128
EXPERTS = 32
TOP = 4
DRAFT_TOKENS = 64
CAP = 24
BLOCK_ROWS = 128


eps_norm = 1e-06
rope_base = 1000000.0


def rms_scale(token_rows, gain_vec):
    widened = token_rows.astype(jnp.float32)
    inverse = lax.rsqrt(jnp.mean(widened * widened, axis=-1, keepdims=True) + eps_norm)
    return (widened * inverse * gain_vec).astype(jnp.bfloat16)


def rotate(values, positions):
    row_count = values.shape[0]
    head_count = values.shape[1] // HEAD_SIZE
    half_size = HEAD_SIZE // 2
    reshaped_rows = values.reshape(row_count, head_count, HEAD_SIZE)
    frequency = rope_base ** (-jnp.arange(half_size, dtype=jnp.float32) / half_size)
    angles = positions.astype(jnp.float32)[:, None] * frequency[None, :]
    cosine = jnp.cos(angles)[:, None, :]
    sine_part = jnp.sin(angles)[:, None, :]
    leading = reshaped_rows[..., :half_size]
    second = reshaped_rows[..., half_size:]
    turned = jnp.concatenate(
        [leading * cosine - second * sine_part, second * cosine + leading * sine_part], axis=-1
    )
    return turned.reshape(row_count, head_count * HEAD_SIZE)


def ancestry(parents):
    node_count = parents.shape[-1]
    node_index = jnp.arange(node_count, dtype=jnp.int32)
    parent_step = (parents[..., :, None] == node_index[None, None, :]).astype(jnp.float32)
    closure = jnp.maximum(parent_step, jnp.eye(node_count, dtype=jnp.float32)[None])
    for squaring in range(max(1, (node_count - 1).bit_length())):
        closure = jnp.minimum(jnp.einsum("rij,rjk->rik", closure, closure), 1.0)
    tree_depth = jnp.sum(closure, axis=-1).astype(jnp.int32) - 1
    return (closure, tree_depth)


def attend(query_rows, tree_key_value, cached_row_block, length, closure):
    tree_drafts = query_rows.shape[0]
    queries_per_group = QUERY_HEADS // KEY_VALUE_HEADS
    key_value_width = KEY_VALUE_HEADS * HEAD_SIZE
    reshaped_rows = query_rows.reshape(tree_drafts, KEY_VALUE_HEADS, queries_per_group, HEAD_SIZE)
    cached_key_rows = cached_row_block[:, :key_value_width].reshape(-1, KEY_VALUE_HEADS, HEAD_SIZE)
    cached_value_rows = cached_row_block[:, key_value_width:].reshape(
        -1, KEY_VALUE_HEADS, HEAD_SIZE
    )
    tree_key_rows = tree_key_value[:, :key_value_width].reshape(-1, KEY_VALUE_HEADS, HEAD_SIZE)
    tree_value_rows = tree_key_value[:, key_value_width:].reshape(-1, KEY_VALUE_HEADS, HEAD_SIZE)
    scale = 1.0 / math.sqrt(HEAD_SIZE)
    cache_scores = (
        jnp.einsum(
            "igsd,jgd->gsij", reshaped_rows, cached_key_rows, preferred_element_type=jnp.float32
        )
        * scale
    )
    draft_scores = (
        jnp.einsum(
            "igsd,jgd->gsij", reshaped_rows, tree_key_rows, preferred_element_type=jnp.float32
        )
        * scale
    )
    live_cache = (jnp.arange(cached_row_block.shape[0]) < length)[None, None, None, :]
    live_draft = (closure > 0.5)[None, None, :, :]
    cache_scores = jnp.where(live_cache, cache_scores, -1e30)
    draft_scores = jnp.where(live_draft, draft_scores, -1e30)
    highest = jnp.maximum(jnp.max(cache_scores, axis=-1), jnp.max(draft_scores, axis=-1))[..., None]
    cache_weight = jnp.exp(cache_scores - highest)
    draft_weight = jnp.exp(draft_scores - highest)
    running = jnp.sum(cache_weight, axis=-1, keepdims=True) + jnp.sum(
        draft_weight, axis=-1, keepdims=True
    )
    cache_probs = (cache_weight / running).astype(jnp.bfloat16)
    draft_probs = (draft_weight / running).astype(jnp.bfloat16)
    context = jnp.einsum(
        "gsij,jgd->igsd", cache_probs, cached_value_rows, preferred_element_type=jnp.float32
    )
    context = context + jnp.einsum(
        "gsij,jgd->igsd", draft_probs, tree_value_rows, preferred_element_type=jnp.float32
    )
    return context.reshape(tree_drafts, QUERY_HEADS * HEAD_SIZE).astype(jnp.bfloat16)


def compact(kv_rows, closure, tree_depth, accepted):
    path_mask = jnp.take_along_axis(closure, accepted[:, None, None], axis=1)[:, 0, :]
    level = jnp.arange(kv_rows.shape[1], dtype=jnp.int32)
    select = (
        path_mask[:, None, :] * (tree_depth[:, None, :] == level[None, :, None]).astype(jnp.float32)
    ).astype(jnp.bfloat16)
    return jnp.einsum("rtj,rjw->rtw", select, kv_rows, preferred_element_type=jnp.float32).astype(
        jnp.bfloat16
    )


def slot_tables(routes, capacity):
    rows = routes.shape[0]
    expert_ids = jnp.arange(EXPERTS, dtype=jnp.int32)
    picks = routes[:, :, None] == expert_ids[None, None, :]
    chosen = jnp.sum(picks.astype(jnp.int32), axis=1).astype(jnp.bfloat16)
    row_ids = jnp.arange(rows, dtype=jnp.int32)
    before = (row_ids[None, :] < row_ids[:, None]).astype(jnp.bfloat16)
    earlier = jnp.dot(before, chosen, preferred_element_type=jnp.float32).astype(jnp.int32)
    slot_number = jnp.sum(jnp.where(picks, earlier[:, None, :], 0), axis=2)
    slot_index = routes * capacity + slot_number
    slot_ids = jnp.arange(EXPERTS * capacity, dtype=jnp.int32)
    hit = slot_index[:, :, None] == slot_ids[None, None, :]
    return hit


def pack_slots(token_rows, hit):
    place = jnp.sum(hit.astype(jnp.bfloat16), axis=1)
    return jnp.einsum("ts,td->sd", place, token_rows, preferred_element_type=jnp.bfloat16)


def expert_products(received, w_gate, w_up, w_down):
    gate_part = jnp.einsum("pekd,edf->pekf", received, w_gate, preferred_element_type=jnp.float32)
    up_part = jnp.einsum("pekd,edf->pekf", received, w_up, preferred_element_type=jnp.float32)
    hidden = (jnp.maximum(gate_part, 0.0) * up_part).astype(jnp.bfloat16)
    return jnp.einsum("pekf,efd->pekd", hidden, w_down, preferred_element_type=jnp.float32).astype(
        jnp.bfloat16
    )


def combine_picks(returned_rows, hit, gate_weights):
    layer_width = returned_rows.shape[-1]
    flat_rows = returned_rows.reshape(-1, layer_width)
    weight = jnp.sum(jnp.where(hit, gate_weights[:, :, None], 0.0), axis=1)
    weight_hi = weight.astype(jnp.bfloat16)
    weight_lo = (weight - weight_hi.astype(jnp.float32)).astype(jnp.bfloat16)
    mixed = jnp.dot(weight_hi, flat_rows, preferred_element_type=jnp.float32)
    return mixed + jnp.dot(weight_lo, flat_rows, preferred_element_type=jnp.float32)


def routed_whole(moe_in, routes, gate_weights, w_gate, w_up, w_down):
    capacity = CAP * (moe_in.shape[0] // BLOCK_ROWS)
    hit = slot_tables(routes, capacity)
    buffer = pack_slots(moe_in, hit)
    peer_count = lax.axis_size("exp")
    reshaped_rows = buffer.reshape(peer_count, w_gate.shape[0], capacity, moe_in.shape[1])
    produced = expert_products(
        lax.all_to_all(reshaped_rows, "exp", split_axis=0, concat_axis=0, tiled=True),
        w_gate,
        w_up,
        w_down,
    )
    returned_rows = lax.all_to_all(produced, "exp", split_axis=0, concat_axis=0, tiled=True)
    return combine_picks(returned_rows, hit, gate_weights)


def relative_gather(shard, axis, plane_count, core_count):
    pieces = [shard]
    for shift in range(1, plane_count):
        pairs = [
            (p * core_count + c, ((p + shift) % plane_count) * core_count + c)
            for p in range(plane_count)
            for c in range(core_count)
        ]
        pieces.append(lax.ppermute(shard, "req", pairs))
    mine = jnp.concatenate(pieces, axis=axis)
    swap = [
        (p * core_count + c, p * core_count + (core_count - 1 - c))
        for p in range(plane_count)
        for c in range(core_count)
    ]
    return jnp.concatenate([mine, lax.ppermute(mine, "req", swap)], axis=axis)


def local(
    tokens,
    attn_gain,
    w_query,
    key_projection,
    value_projection,
    w_out,
    moe_gain,
    w_gate,
    w_up,
    w_down,
    routes,
    gate_weights,
    kv_cache,
    lengths,
    parents,
    accepted,
):
    rows_here = tokens.shape[0]
    local_reqs = kv_cache.shape[0]
    normed = rms_scale(tokens, attn_gain)
    closure, tree_depth = ancestry(parents)
    positions = (lengths[:, None] + tree_depth).reshape(-1)
    core_count = 2
    plane_count = lax.axis_size("req") // core_count
    place = lax.axis_index("req")
    plane_me, core_me = place // core_count, place % core_count
    plane_order = (plane_me - jnp.arange(plane_count, dtype=jnp.int32)) % plane_count
    joined = jnp.concatenate([w_query, key_projection, value_projection], axis=1)
    gathered = relative_gather(joined, 0, plane_count, core_count)
    shard_rows = w_query.shape[0]
    blocks = normed.reshape(rows_here, plane_count, core_count, shard_rows)
    blocks = jnp.where(core_me == 0, blocks, blocks[:, :, ::-1])
    normed_perm = (
        jnp.take(blocks, plane_order, axis=1).transpose(0, 2, 1, 3).reshape(rows_here, -1)
    )
    qkv_sum = jnp.dot(normed_perm, gathered, preferred_element_type=jnp.float32)
    query_width = w_query.shape[1]
    kv_width = key_projection.shape[1]
    query_sum = qkv_sum[:, :query_width]
    key_sum = qkv_sum[:, query_width : query_width + kv_width]
    value_sum = qkv_sum[:, query_width + kv_width :]
    query_rows = rotate(query_sum, positions).astype(jnp.bfloat16)
    tree_key_value = jnp.concatenate([rotate(key_sum, positions), value_sum], axis=1).astype(
        jnp.bfloat16
    )
    query_req = query_rows.reshape(local_reqs, DRAFT_TOKENS, query_rows.shape[1])
    key_value_request = tree_key_value.reshape(local_reqs, DRAFT_TOKENS, tree_key_value.shape[1])
    out_cols = w_out.shape[1]
    w_out_after, _ = lax.optimization_barrier((w_out, gathered))
    w_out_full = relative_gather(w_out_after, 1, plane_count, core_count)
    chunk_count = rows_here // BLOCK_ROWS
    reqs_per_chunk = local_reqs // chunk_count
    outs = []
    for chunk in range(chunk_count):
        rq = slice(chunk * reqs_per_chunk, (chunk + 1) * reqs_per_chunk)
        rw = slice(chunk * BLOCK_ROWS, (chunk + 1) * BLOCK_ROWS)
        context = jax.vmap(attend)(
            query_req[rq], key_value_request[rq], kv_cache[rq], lengths[rq], closure[rq]
        ).reshape(BLOCK_ROWS, -1)
        attn_rel = jnp.dot(context, w_out_full, preferred_element_type=jnp.float32).reshape(
            BLOCK_ROWS, core_count, plane_count, out_cols
        )
        attn_rel = jnp.where(core_me == 0, attn_rel, attn_rel[:, ::-1])
        attn_out = (
            jnp.take(attn_rel, plane_order, axis=2).transpose(0, 2, 1, 3).reshape(BLOCK_ROWS, -1)
        )
        residual = (tokens[rw].astype(jnp.float32) + attn_out).astype(jnp.bfloat16)
        moe_in = rms_scale(residual, moe_gain)
        mixed = routed_whole(moe_in, routes[rw], gate_weights[rw], w_gate, w_up, w_down)
        outs.append((residual.astype(jnp.float32) + mixed).astype(jnp.bfloat16))
    layer_out = jnp.concatenate(outs, axis=0)
    new_entries = compact(key_value_request, closure, tree_depth, accepted)
    return (layer_out, new_entries)


def solution(mesh):
    return jax.shard_map(
        local,
        mesh=mesh,
        in_specs=(
            P(("req", "exp"), None),
            P(),
            P("req", None),
            P("req", None),
            P("req", None),
            P(None, "req"),
            P(),
            P("exp", None, None),
            P("exp", None, None),
            P("exp", None, None),
            P(("req", "exp"), None),
            P(("req", "exp"), None),
            P(("req", "exp"), None, None),
            P(("req", "exp")),
            P(("req", "exp"), None),
            P(("req", "exp")),
        ),
        out_specs=(P(("req", "exp"), None), P(("req", "exp"), None, None)),
        check_vma=False,
    )
```

```python
import math

import jax
import jax.numpy as jnp
from jax import lax
from jax.sharding import PartitionSpec as P

QUERY_HEADS = 12
KEY_VALUE_HEADS = 2
HEAD_SIZE = 128
EXPERTS = 32
TOP = 4
DRAFT_TOKENS = 64
CAP = 24
BLOCK_ROWS = 128


eps_norm = 1e-06
rope_base = 1000000.0


def rms_scale(token_rows, gain_vec):
    widened = token_rows.astype(jnp.float32)
    inverse = lax.rsqrt(jnp.mean(widened * widened, axis=-1, keepdims=True) + eps_norm)
    return (widened * inverse * gain_vec).astype(jnp.bfloat16)


def rotate(values, positions):
    row_count = values.shape[0]
    head_count = values.shape[1] // HEAD_SIZE
    half_size = HEAD_SIZE // 2
    reshaped_rows = values.reshape(row_count, head_count, HEAD_SIZE)
    frequency = rope_base ** (-jnp.arange(half_size, dtype=jnp.float32) / half_size)
    angles = positions.astype(jnp.float32)[:, None] * frequency[None, :]
    cosine = jnp.cos(angles)[:, None, :]
    sine_part = jnp.sin(angles)[:, None, :]
    leading = reshaped_rows[..., :half_size]
    second = reshaped_rows[..., half_size:]
    turned = jnp.concatenate(
        [leading * cosine - second * sine_part, second * cosine + leading * sine_part], axis=-1
    )
    return turned.reshape(row_count, head_count * HEAD_SIZE)


def ancestry(parents):
    node_count = parents.shape[-1]
    node_index = jnp.arange(node_count, dtype=jnp.int32)
    parent_step = (parents[..., :, None] == node_index[None, None, :]).astype(jnp.float32)
    closure = jnp.maximum(parent_step, jnp.eye(node_count, dtype=jnp.float32)[None])
    for squaring in range(max(1, (node_count - 1).bit_length())):
        closure = jnp.minimum(jnp.einsum("rij,rjk->rik", closure, closure), 1.0)
    tree_depth = jnp.sum(closure, axis=-1).astype(jnp.int32) - 1
    return (closure, tree_depth)


def attend(query_rows, tree_key_value, cached_row_block, length, closure):
    tree_drafts = query_rows.shape[0]
    queries_per_group = QUERY_HEADS // KEY_VALUE_HEADS
    key_value_width = KEY_VALUE_HEADS * HEAD_SIZE
    reshaped_rows = query_rows.reshape(tree_drafts, KEY_VALUE_HEADS, queries_per_group, HEAD_SIZE)
    cached_key_rows = cached_row_block[:, :key_value_width].reshape(-1, KEY_VALUE_HEADS, HEAD_SIZE)
    cached_value_rows = cached_row_block[:, key_value_width:].reshape(
        -1, KEY_VALUE_HEADS, HEAD_SIZE
    )
    tree_key_rows = tree_key_value[:, :key_value_width].reshape(-1, KEY_VALUE_HEADS, HEAD_SIZE)
    tree_value_rows = tree_key_value[:, key_value_width:].reshape(-1, KEY_VALUE_HEADS, HEAD_SIZE)
    scale = 1.0 / math.sqrt(HEAD_SIZE)
    cache_scores = (
        jnp.einsum(
            "igsd,jgd->gsij", reshaped_rows, cached_key_rows, preferred_element_type=jnp.float32
        )
        * scale
    )
    draft_scores = (
        jnp.einsum(
            "igsd,jgd->gsij", reshaped_rows, tree_key_rows, preferred_element_type=jnp.float32
        )
        * scale
    )
    live_cache = (jnp.arange(cached_row_block.shape[0]) < length)[None, None, None, :]
    live_draft = (closure > 0.5)[None, None, :, :]
    cache_scores = jnp.where(live_cache, cache_scores, -1e30)
    draft_scores = jnp.where(live_draft, draft_scores, -1e30)
    highest = jnp.maximum(jnp.max(cache_scores, axis=-1), jnp.max(draft_scores, axis=-1))[..., None]
    cache_weight = jnp.exp(cache_scores - highest)
    draft_weight = jnp.exp(draft_scores - highest)
    running = jnp.sum(cache_weight, axis=-1, keepdims=True) + jnp.sum(
        draft_weight, axis=-1, keepdims=True
    )
    cache_probs = (cache_weight / running).astype(jnp.bfloat16)
    draft_probs = (draft_weight / running).astype(jnp.bfloat16)
    context = jnp.einsum(
        "gsij,jgd->igsd", cache_probs, cached_value_rows, preferred_element_type=jnp.float32
    )
    context = context + jnp.einsum(
        "gsij,jgd->igsd", draft_probs, tree_value_rows, preferred_element_type=jnp.float32
    )
    return context.reshape(tree_drafts, QUERY_HEADS * HEAD_SIZE).astype(jnp.bfloat16)


def compact(kv_rows, closure, tree_depth, accepted):
    path_mask = jnp.take_along_axis(closure, accepted[:, None, None], axis=1)[:, 0, :]
    level = jnp.arange(kv_rows.shape[1], dtype=jnp.int32)
    select = (
        path_mask[:, None, :] * (tree_depth[:, None, :] == level[None, :, None]).astype(jnp.float32)
    ).astype(jnp.bfloat16)
    return jnp.einsum("rtj,rjw->rtw", select, kv_rows, preferred_element_type=jnp.float32).astype(
        jnp.bfloat16
    )


def slot_tables(routes, capacity):
    rows = routes.shape[0]
    expert_ids = jnp.arange(EXPERTS, dtype=jnp.int32)
    picks = routes[:, :, None] == expert_ids[None, None, :]
    chosen = jnp.sum(picks.astype(jnp.int32), axis=1).astype(jnp.bfloat16)
    row_ids = jnp.arange(rows, dtype=jnp.int32)
    before = (row_ids[None, :] < row_ids[:, None]).astype(jnp.bfloat16)
    earlier = jnp.dot(before, chosen, preferred_element_type=jnp.float32).astype(jnp.int32)
    slot_number = jnp.sum(jnp.where(picks, earlier[:, None, :], 0), axis=2)
    slot_index = routes * capacity + slot_number
    slot_ids = jnp.arange(EXPERTS * capacity, dtype=jnp.int32)
    hit = slot_index[:, :, None] == slot_ids[None, None, :]
    return hit


def pack_slots(token_rows, hit):
    place = jnp.sum(hit.astype(jnp.bfloat16), axis=1)
    return jnp.einsum("ts,td->sd", place, token_rows, preferred_element_type=jnp.bfloat16)


def expert_products(received, w_gate, w_up, w_down):
    gate_part = jnp.einsum("pekd,edf->pekf", received, w_gate, preferred_element_type=jnp.float32)
    up_part = jnp.einsum("pekd,edf->pekf", received, w_up, preferred_element_type=jnp.float32)
    hidden = (jnp.maximum(gate_part, 0.0) * up_part).astype(jnp.bfloat16)
    return jnp.einsum("pekf,efd->pekd", hidden, w_down, preferred_element_type=jnp.float32).astype(
        jnp.bfloat16
    )


def combine_picks(returned_rows, hit, gate_weights):
    layer_width = returned_rows.shape[-1]
    flat_rows = returned_rows.reshape(-1, layer_width)
    weight = jnp.sum(jnp.where(hit, gate_weights[:, :, None], 0.0), axis=1)
    weight_hi = weight.astype(jnp.bfloat16)
    weight_lo = (weight - weight_hi.astype(jnp.float32)).astype(jnp.bfloat16)
    mixed = jnp.dot(weight_hi, flat_rows, preferred_element_type=jnp.float32)
    return mixed + jnp.dot(weight_lo, flat_rows, preferred_element_type=jnp.float32)


def routed_whole(moe_in, routes, gate_weights, w_gate, w_up, w_down):
    capacity = CAP * (moe_in.shape[0] // BLOCK_ROWS)
    hit = slot_tables(routes, capacity)
    buffer = pack_slots(moe_in, hit)
    peer_count = lax.axis_size("exp")
    reshaped_rows = buffer.reshape(peer_count, w_gate.shape[0], capacity, moe_in.shape[1])
    produced = expert_products(
        lax.all_to_all(reshaped_rows, "exp", split_axis=0, concat_axis=0, tiled=True),
        w_gate,
        w_up,
        w_down,
    )
    returned_rows = lax.all_to_all(produced, "exp", split_axis=0, concat_axis=0, tiled=True)
    return combine_picks(returned_rows, hit, gate_weights)


def local(
    tokens,
    attn_gain,
    w_query,
    key_projection,
    value_projection,
    w_out,
    moe_gain,
    w_gate,
    w_up,
    w_down,
    routes,
    gate_weights,
    kv_cache,
    lengths,
    parents,
    accepted,
):
    rows_here = tokens.shape[0]
    local_reqs = kv_cache.shape[0]
    normed = rms_scale(tokens, attn_gain)
    closure, tree_depth = ancestry(parents)
    positions = (lengths[:, None] + tree_depth).reshape(-1)
    query_sum = jnp.dot(
        normed,
        lax.all_gather(w_query, "req", axis=0, tiled=True),
        preferred_element_type=jnp.float32,
    )
    key_sum = jnp.dot(
        normed,
        lax.all_gather(key_projection, "req", axis=0, tiled=True),
        preferred_element_type=jnp.float32,
    )
    value_sum = jnp.dot(
        normed,
        lax.all_gather(value_projection, "req", axis=0, tiled=True),
        preferred_element_type=jnp.float32,
    )
    query_rows = rotate(query_sum, positions).astype(jnp.bfloat16)
    tree_key_value = jnp.concatenate([rotate(key_sum, positions), value_sum], axis=1).astype(
        jnp.bfloat16
    )
    query_req = query_rows.reshape(local_reqs, DRAFT_TOKENS, query_rows.shape[1])
    key_value_request = tree_key_value.reshape(local_reqs, DRAFT_TOKENS, tree_key_value.shape[1])
    w_out_full = lax.all_gather(w_out, "req", axis=1, tiled=True)
    chunk_count = rows_here // BLOCK_ROWS
    context_all = jax.vmap(attend)(
        query_req, key_value_request, kv_cache, lengths, closure
    ).reshape(rows_here, -1)
    outs = []
    for chunk in range(chunk_count):
        rw = slice(chunk * BLOCK_ROWS, (chunk + 1) * BLOCK_ROWS)
        attn_out = jnp.dot(context_all[rw], w_out_full, preferred_element_type=jnp.float32)
        residual = (tokens[rw].astype(jnp.float32) + attn_out).astype(jnp.bfloat16)
        moe_in = rms_scale(residual, moe_gain)
        mixed = routed_whole(moe_in, routes[rw], gate_weights[rw], w_gate, w_up, w_down)
        outs.append((residual.astype(jnp.float32) + mixed).astype(jnp.bfloat16))
    layer_out = jnp.concatenate(outs, axis=0)
    new_entries = compact(key_value_request, closure, tree_depth, accepted)
    return (layer_out, new_entries)


def solution(mesh):
    return jax.shard_map(
        local,
        mesh=mesh,
        in_specs=(
            P(("req", "exp"), None),
            P(),
            P("req", None),
            P("req", None),
            P("req", None),
            P(None, "req"),
            P(),
            P("exp", None, None),
            P("exp", None, None),
            P("exp", None, None),
            P(("req", "exp"), None),
            P(("req", "exp"), None),
            P(("req", "exp"), None, None),
            P(("req", "exp")),
            P(("req", "exp"), None),
            P(("req", "exp")),
        ),
        out_specs=(P(("req", "exp"), None), P(("req", "exp"), None, None)),
        check_vma=False,
    )
```

```python
import math

import jax
import jax.numpy as jnp
from jax import lax
from jax.sharding import PartitionSpec as P

QUERY_HEADS = 12
KEY_VALUE_HEADS = 2
HEAD_SIZE = 128
EXPERTS = 32
TOP = 4
DRAFT_TOKENS = 64
CAP = 24
BLOCK_ROWS = 128


eps_norm = 1e-06
rope_base = 1000000.0


def rms_scale(token_rows, gain_vec):
    widened = token_rows.astype(jnp.float32)
    inverse = lax.rsqrt(jnp.mean(widened * widened, axis=-1, keepdims=True) + eps_norm)
    return (widened * inverse * gain_vec).astype(jnp.bfloat16)


def rotate(values, positions):
    row_count = values.shape[0]
    head_count = values.shape[1] // HEAD_SIZE
    half_size = HEAD_SIZE // 2
    reshaped_rows = values.reshape(row_count, head_count, HEAD_SIZE)
    frequency = rope_base ** (-jnp.arange(half_size, dtype=jnp.float32) / half_size)
    angles = positions.astype(jnp.float32)[:, None] * frequency[None, :]
    cosine = jnp.cos(angles)[:, None, :]
    sine_part = jnp.sin(angles)[:, None, :]
    leading = reshaped_rows[..., :half_size]
    second = reshaped_rows[..., half_size:]
    turned = jnp.concatenate(
        [leading * cosine - second * sine_part, second * cosine + leading * sine_part], axis=-1
    )
    return turned.reshape(row_count, head_count * HEAD_SIZE)


def ancestry(parents):
    node_count = parents.shape[-1]
    node_index = jnp.arange(node_count, dtype=jnp.int32)
    parent_step = (parents[..., :, None] == node_index[None, None, :]).astype(jnp.float32)
    closure = jnp.maximum(parent_step, jnp.eye(node_count, dtype=jnp.float32)[None])
    for squaring in range(max(1, (node_count - 1).bit_length())):
        closure = jnp.minimum(jnp.einsum("rij,rjk->rik", closure, closure), 1.0)
    tree_depth = jnp.sum(closure, axis=-1).astype(jnp.int32) - 1
    return (closure, tree_depth)


def attend(query_rows, tree_key_value, cached_row_block, length, closure):
    tree_drafts = query_rows.shape[0]
    queries_per_group = QUERY_HEADS // KEY_VALUE_HEADS
    key_value_width = KEY_VALUE_HEADS * HEAD_SIZE
    reshaped_rows = query_rows.reshape(tree_drafts, KEY_VALUE_HEADS, queries_per_group, HEAD_SIZE)
    cached_key_rows = cached_row_block[:, :key_value_width].reshape(-1, KEY_VALUE_HEADS, HEAD_SIZE)
    cached_value_rows = cached_row_block[:, key_value_width:].reshape(
        -1, KEY_VALUE_HEADS, HEAD_SIZE
    )
    tree_key_rows = tree_key_value[:, :key_value_width].reshape(-1, KEY_VALUE_HEADS, HEAD_SIZE)
    tree_value_rows = tree_key_value[:, key_value_width:].reshape(-1, KEY_VALUE_HEADS, HEAD_SIZE)
    scale = 1.0 / math.sqrt(HEAD_SIZE)
    cache_scores = (
        jnp.einsum(
            "igsd,jgd->gsij", reshaped_rows, cached_key_rows, preferred_element_type=jnp.float32
        )
        * scale
    )
    draft_scores = (
        jnp.einsum(
            "igsd,jgd->gsij", reshaped_rows, tree_key_rows, preferred_element_type=jnp.float32
        )
        * scale
    )
    live_cache = (jnp.arange(cached_row_block.shape[0]) < length)[None, None, None, :]
    live_draft = (closure > 0.5)[None, None, :, :]
    cache_scores = jnp.where(live_cache, cache_scores, -1e30)
    draft_scores = jnp.where(live_draft, draft_scores, -1e30)
    highest = jnp.maximum(jnp.max(cache_scores, axis=-1), jnp.max(draft_scores, axis=-1))[..., None]
    cache_weight = jnp.exp(cache_scores - highest)
    draft_weight = jnp.exp(draft_scores - highest)
    running = jnp.sum(cache_weight, axis=-1, keepdims=True) + jnp.sum(
        draft_weight, axis=-1, keepdims=True
    )
    cache_probs = (cache_weight / running).astype(jnp.bfloat16)
    draft_probs = (draft_weight / running).astype(jnp.bfloat16)
    context = jnp.einsum(
        "gsij,jgd->igsd", cache_probs, cached_value_rows, preferred_element_type=jnp.float32
    )
    context = context + jnp.einsum(
        "gsij,jgd->igsd", draft_probs, tree_value_rows, preferred_element_type=jnp.float32
    )
    return context.reshape(tree_drafts, QUERY_HEADS * HEAD_SIZE).astype(jnp.bfloat16)


def compact(kv_rows, closure, tree_depth, accepted):
    path_mask = jnp.take_along_axis(closure, accepted[:, None, None], axis=1)[:, 0, :]
    level = jnp.arange(kv_rows.shape[1], dtype=jnp.int32)
    select = (
        path_mask[:, None, :] * (tree_depth[:, None, :] == level[None, :, None]).astype(jnp.float32)
    ).astype(jnp.bfloat16)
    return jnp.einsum("rtj,rjw->rtw", select, kv_rows, preferred_element_type=jnp.float32).astype(
        jnp.bfloat16
    )


def slot_tables(routes, gate_weights, capacity):
    rows = routes.shape[0]
    expert_ids = jnp.arange(EXPERTS, dtype=jnp.int32)
    picks = routes[:, :, None] == expert_ids[None, None, :]
    chosen = jnp.sum(picks.astype(jnp.int32), axis=1).astype(jnp.bfloat16)
    row_ids = jnp.arange(rows, dtype=jnp.int32)
    same_block = (row_ids[None, :] // BLOCK_ROWS) == (row_ids[:, None] // BLOCK_ROWS)
    before = ((row_ids[None, :] < row_ids[:, None]) & same_block).astype(jnp.bfloat16)
    earlier = jnp.dot(before, chosen, preferred_element_type=jnp.float32).astype(jnp.int32)
    slot_number = jnp.sum(jnp.where(picks, earlier[:, None, :], 0), axis=2)
    slot_index = routes * capacity + slot_number
    slot_ids = jnp.arange(EXPERTS * capacity, dtype=jnp.int32)
    hit = slot_index[:, :, None] == slot_ids[None, None, :]
    place = jnp.sum(hit.astype(jnp.bfloat16), axis=1)
    weight = jnp.sum(jnp.where(hit, gate_weights[:, :, None], 0.0), axis=1)
    weight_hi = weight.astype(jnp.bfloat16)
    weight_lo = (weight - weight_hi.astype(jnp.float32)).astype(jnp.bfloat16)
    return place, weight_hi, weight_lo


def pack_slots(token_rows, place):
    return jnp.einsum("ts,td->sd", place, token_rows, preferred_element_type=jnp.bfloat16)


def expert_products(received, w_gate, w_up, w_down):
    gate_part = jnp.einsum("pekd,edf->pekf", received, w_gate, preferred_element_type=jnp.float32)
    up_part = jnp.einsum("pekd,edf->pekf", received, w_up, preferred_element_type=jnp.float32)
    hidden = (jnp.maximum(gate_part, 0.0) * up_part).astype(jnp.bfloat16)
    return jnp.einsum("pekf,efd->pekd", hidden, w_down, preferred_element_type=jnp.float32).astype(
        jnp.bfloat16
    )


def combine_picks(returned_rows, weight_hi, weight_lo):
    layer_width = returned_rows.shape[-1]
    rows = weight_hi.shape[0]
    flat_rows = returned_rows.reshape(-1, layer_width)
    both = jnp.concatenate([weight_hi, weight_lo], axis=0)
    mixed = jnp.dot(both, flat_rows, preferred_element_type=jnp.float32)
    return mixed[:rows] + mixed[rows:]


def routed_whole(moe_in, place, weight_hi, weight_lo, w_gate, w_up, w_down):
    capacity = place.shape[1] // EXPERTS
    buffer = pack_slots(moe_in, place)
    peer_count = lax.axis_size("exp")
    reshaped_rows = buffer.reshape(peer_count, w_gate.shape[0], capacity, moe_in.shape[1])
    produced = expert_products(
        lax.all_to_all(reshaped_rows, "exp", split_axis=0, concat_axis=0, tiled=True),
        w_gate,
        w_up,
        w_down,
    )
    returned_rows = lax.all_to_all(produced, "exp", split_axis=0, concat_axis=0, tiled=True)
    return combine_picks(returned_rows, weight_hi, weight_lo)


def local(
    tokens,
    attn_gain,
    w_query,
    key_projection,
    value_projection,
    w_out,
    moe_gain,
    w_gate,
    w_up,
    w_down,
    routes,
    gate_weights,
    kv_cache,
    lengths,
    parents,
    accepted,
):
    rows_here = tokens.shape[0]
    local_reqs = kv_cache.shape[0]
    normed = rms_scale(tokens, attn_gain)
    closure, tree_depth = ancestry(parents)
    positions = (lengths[:, None] + tree_depth).reshape(-1)
    query_sum = jnp.dot(
        normed,
        lax.all_gather(w_query, "req", axis=0, tiled=True),
        preferred_element_type=jnp.float32,
    )
    key_sum = jnp.dot(
        normed,
        lax.all_gather(key_projection, "req", axis=0, tiled=True),
        preferred_element_type=jnp.float32,
    )
    value_sum = jnp.dot(
        normed,
        lax.all_gather(value_projection, "req", axis=0, tiled=True),
        preferred_element_type=jnp.float32,
    )
    query_rows = rotate(query_sum, positions).astype(jnp.bfloat16)
    tree_key_value = jnp.concatenate([rotate(key_sum, positions), value_sum], axis=1).astype(
        jnp.bfloat16
    )
    query_req = query_rows.reshape(local_reqs, DRAFT_TOKENS, query_rows.shape[1])
    key_value_request = tree_key_value.reshape(local_reqs, DRAFT_TOKENS, tree_key_value.shape[1])
    w_out_full = lax.all_gather(w_out, "req", axis=1, tiled=True)
    chunk_count = rows_here // BLOCK_ROWS
    context_all = jax.vmap(attend)(
        query_req, key_value_request, kv_cache, lengths, closure
    ).reshape(rows_here, -1)
    place, weight_hi, weight_lo = slot_tables(routes, gate_weights, CAP)
    outs = []
    for chunk in range(chunk_count):
        rw = slice(chunk * BLOCK_ROWS, (chunk + 1) * BLOCK_ROWS)
        attn_out = jnp.dot(context_all[rw], w_out_full, preferred_element_type=jnp.float32)
        residual = (tokens[rw].astype(jnp.float32) + attn_out).astype(jnp.bfloat16)
        moe_in = rms_scale(residual, moe_gain)
        mixed = routed_whole(
            moe_in, place[rw], weight_hi[rw], weight_lo[rw], w_gate, w_up, w_down
        )
        outs.append((residual.astype(jnp.float32) + mixed).astype(jnp.bfloat16))
    layer_out = jnp.concatenate(outs, axis=0)
    new_entries = compact(key_value_request, closure, tree_depth, accepted)
    return (layer_out, new_entries)


def solution(mesh):
    return jax.shard_map(
        local,
        mesh=mesh,
        in_specs=(
            P(("req", "exp"), None),
            P(),
            P("req", None),
            P("req", None),
            P("req", None),
            P(None, "req"),
            P(),
            P("exp", None, None),
            P("exp", None, None),
            P("exp", None, None),
            P(("req", "exp"), None),
            P(("req", "exp"), None),
            P(("req", "exp"), None, None),
            P(("req", "exp")),
            P(("req", "exp"), None),
            P(("req", "exp")),
        ),
        out_specs=(P(("req", "exp"), None), P(("req", "exp"), None, None)),
        check_vma=False,
    )
```

```python
import math

import jax
import jax.numpy as jnp
from jax import lax
from jax.sharding import PartitionSpec as P

QUERY_HEADS = 12
KEY_VALUE_HEADS = 2
HEAD_SIZE = 128
EXPERTS = 32
TOP = 4
DRAFT_TOKENS = 64
CAP = 24
BLOCK_ROWS = 128


eps_norm = 1e-06
rope_base = 1000000.0


def rms_scale(token_rows, gain_vec):
    widened = token_rows.astype(jnp.float32)
    inverse = lax.rsqrt(jnp.mean(widened * widened, axis=-1, keepdims=True) + eps_norm)
    return (widened * inverse * gain_vec).astype(jnp.bfloat16)


def rotate(values, positions):
    row_count = values.shape[0]
    head_count = values.shape[1] // HEAD_SIZE
    half_size = HEAD_SIZE // 2
    reshaped_rows = values.reshape(row_count, head_count, HEAD_SIZE)
    frequency = rope_base ** (-jnp.arange(half_size, dtype=jnp.float32) / half_size)
    angles = positions.astype(jnp.float32)[:, None] * frequency[None, :]
    cosine = jnp.cos(angles)[:, None, :]
    sine_part = jnp.sin(angles)[:, None, :]
    leading = reshaped_rows[..., :half_size]
    second = reshaped_rows[..., half_size:]
    turned = jnp.concatenate(
        [leading * cosine - second * sine_part, second * cosine + leading * sine_part], axis=-1
    )
    return turned.reshape(row_count, head_count * HEAD_SIZE)


def ancestry(parents):
    node_count = parents.shape[-1]
    node_index = jnp.arange(node_count, dtype=jnp.int32)
    parent_step = (parents[..., :, None] == node_index[None, None, :]).astype(jnp.float32)
    closure = jnp.maximum(parent_step, jnp.eye(node_count, dtype=jnp.float32)[None])
    for squaring in range(max(1, (node_count - 1).bit_length())):
        closure = jnp.minimum(jnp.einsum("rij,rjk->rik", closure, closure), 1.0)
    tree_depth = jnp.sum(closure, axis=-1).astype(jnp.int32) - 1
    return (closure, tree_depth)


def attend(query_rows, tree_key_value, cached_row_block, length, closure):
    tree_drafts = query_rows.shape[0]
    queries_per_group = QUERY_HEADS // KEY_VALUE_HEADS
    key_value_width = KEY_VALUE_HEADS * HEAD_SIZE
    reshaped_rows = query_rows.reshape(tree_drafts, KEY_VALUE_HEADS, queries_per_group, HEAD_SIZE)
    cached_key_rows = cached_row_block[:, :key_value_width].reshape(-1, KEY_VALUE_HEADS, HEAD_SIZE)
    cached_value_rows = cached_row_block[:, key_value_width:].reshape(
        -1, KEY_VALUE_HEADS, HEAD_SIZE
    )
    tree_key_rows = tree_key_value[:, :key_value_width].reshape(-1, KEY_VALUE_HEADS, HEAD_SIZE)
    tree_value_rows = tree_key_value[:, key_value_width:].reshape(-1, KEY_VALUE_HEADS, HEAD_SIZE)
    scale = 1.0 / math.sqrt(HEAD_SIZE)
    cache_scores = (
        jnp.einsum(
            "igsd,jgd->gsij", reshaped_rows, cached_key_rows, preferred_element_type=jnp.float32
        )
        * scale
    )
    draft_scores = (
        jnp.einsum(
            "igsd,jgd->gsij", reshaped_rows, tree_key_rows, preferred_element_type=jnp.float32
        )
        * scale
    )
    live_cache = (jnp.arange(cached_row_block.shape[0]) < length)[None, None, None, :]
    live_draft = (closure > 0.5)[None, None, :, :]
    cache_scores = jnp.where(live_cache, cache_scores, -1e30)
    draft_scores = jnp.where(live_draft, draft_scores, -1e30)
    highest = jnp.maximum(jnp.max(cache_scores, axis=-1), jnp.max(draft_scores, axis=-1))[..., None]
    cache_weight = jnp.exp(cache_scores - highest)
    draft_weight = jnp.exp(draft_scores - highest)
    running = jnp.sum(cache_weight, axis=-1, keepdims=True) + jnp.sum(
        draft_weight, axis=-1, keepdims=True
    )
    cache_probs = (cache_weight / running).astype(jnp.bfloat16)
    draft_probs = (draft_weight / running).astype(jnp.bfloat16)
    context = jnp.einsum(
        "gsij,jgd->igsd", cache_probs, cached_value_rows, preferred_element_type=jnp.float32
    )
    context = context + jnp.einsum(
        "gsij,jgd->igsd", draft_probs, tree_value_rows, preferred_element_type=jnp.float32
    )
    return context.reshape(tree_drafts, QUERY_HEADS * HEAD_SIZE).astype(jnp.bfloat16)


def compact(kv_rows, closure, tree_depth, accepted):
    path_mask = jnp.take_along_axis(closure, accepted[:, None, None], axis=1)[:, 0, :]
    level = jnp.arange(kv_rows.shape[1], dtype=jnp.int32)
    select = (
        path_mask[:, None, :] * (tree_depth[:, None, :] == level[None, :, None]).astype(jnp.float32)
    ).astype(jnp.bfloat16)
    return jnp.einsum("rtj,rjw->rtw", select, kv_rows, preferred_element_type=jnp.float32).astype(
        jnp.bfloat16
    )


def slot_tables(routes, gate_weights, capacity):
    rows = routes.shape[0]
    expert_ids = jnp.arange(EXPERTS, dtype=jnp.int32)
    picks = routes[:, :, None] == expert_ids[None, None, :]
    chosen = jnp.sum(picks.astype(jnp.int32), axis=1).astype(jnp.bfloat16)
    row_ids = jnp.arange(rows, dtype=jnp.int32)
    same_block = (row_ids[None, :] // BLOCK_ROWS) == (row_ids[:, None] // BLOCK_ROWS)
    before = ((row_ids[None, :] < row_ids[:, None]) & same_block).astype(jnp.bfloat16)
    earlier = jnp.dot(before, chosen, preferred_element_type=jnp.float32).astype(jnp.int32)
    slot_number = jnp.sum(jnp.where(picks, earlier[:, None, :], 0), axis=2)
    slot_index = routes * capacity + slot_number
    slot_ids = jnp.arange(EXPERTS * capacity, dtype=jnp.int32)
    hit = slot_index[:, :, None] == slot_ids[None, None, :]
    place = jnp.sum(hit.astype(jnp.bfloat16), axis=1)
    weight = jnp.sum(jnp.where(hit, gate_weights[:, :, None], 0.0), axis=1)
    weight_hi = weight.astype(jnp.bfloat16)
    weight_lo = (weight - weight_hi.astype(jnp.float32)).astype(jnp.bfloat16)
    return place, weight_hi, weight_lo


def pack_slots(token_rows, place):
    return jnp.einsum("ts,td->sd", place, token_rows, preferred_element_type=jnp.bfloat16)


def expert_products(received, w_gate, w_up, w_down):
    gate_part = jnp.einsum("pekd,edf->pekf", received, w_gate, preferred_element_type=jnp.float32)
    up_part = jnp.einsum("pekd,edf->pekf", received, w_up, preferred_element_type=jnp.float32)
    hidden = (jnp.maximum(gate_part, 0.0) * up_part).astype(jnp.bfloat16)
    return jnp.einsum("pekf,efd->pekd", hidden, w_down, preferred_element_type=jnp.float32).astype(
        jnp.bfloat16
    )


def combine_picks(returned_rows, weight_hi, weight_lo):
    layer_width = returned_rows.shape[-1]
    rows = weight_hi.shape[0]
    flat_rows = returned_rows.reshape(-1, layer_width)
    both = jnp.concatenate([weight_hi, weight_lo], axis=0)
    mixed = jnp.dot(both, flat_rows, preferred_element_type=jnp.float32)
    return mixed[:rows] + mixed[rows:]


def routed_whole(moe_in, place, weight_hi, weight_lo, w_gate, w_up, w_down):
    capacity = place.shape[1] // EXPERTS
    buffer = pack_slots(moe_in, place)
    peer_count = lax.axis_size("exp")
    reshaped_rows = buffer.reshape(peer_count, w_gate.shape[0], capacity, moe_in.shape[1])
    produced = expert_products(
        lax.all_to_all(reshaped_rows, "exp", split_axis=0, concat_axis=0, tiled=True),
        w_gate,
        w_up,
        w_down,
    )
    returned_rows = lax.all_to_all(produced, "exp", split_axis=0, concat_axis=0, tiled=True)
    return combine_picks(returned_rows, weight_hi, weight_lo)


def plane_shift(piece, shift, plane_count, core_count):
    pairs = [
        (p * core_count + c, ((p + shift) % plane_count) * core_count + c)
        for p in range(plane_count)
        for c in range(core_count)
    ]
    return lax.ppermute(piece, "req", pairs)


def balanced_gather(shard, plane_count, core_count):
    half = shard.shape[1] // 2
    from_below = plane_shift(shard, 1, plane_count, core_count)
    from_above = plane_shift(shard, plane_count - 1, plane_count, core_count)
    far_low = plane_shift(from_below[:, :half], 1, plane_count, core_count)
    far_high = plane_shift(from_above[:, half:], plane_count - 1, plane_count, core_count)
    mine = jnp.concatenate([shard, from_below, far_low, far_high, from_above], axis=1)
    swap = [
        (p * core_count + c, p * core_count + (core_count - 1 - c))
        for p in range(plane_count)
        for c in range(core_count)
    ]
    return jnp.concatenate([mine, lax.ppermute(mine, "req", swap)], axis=1)


def local(
    tokens,
    attn_gain,
    w_query,
    key_projection,
    value_projection,
    w_out,
    moe_gain,
    w_gate,
    w_up,
    w_down,
    routes,
    gate_weights,
    kv_cache,
    lengths,
    parents,
    accepted,
):
    rows_here = tokens.shape[0]
    local_reqs = kv_cache.shape[0]
    normed = rms_scale(tokens, attn_gain)
    closure, tree_depth = ancestry(parents)
    positions = (lengths[:, None] + tree_depth).reshape(-1)
    query_sum = jnp.dot(
        normed,
        lax.all_gather(w_query, "req", axis=0, tiled=True),
        preferred_element_type=jnp.float32,
    )
    key_sum = jnp.dot(
        normed,
        lax.all_gather(key_projection, "req", axis=0, tiled=True),
        preferred_element_type=jnp.float32,
    )
    value_sum = jnp.dot(
        normed,
        lax.all_gather(value_projection, "req", axis=0, tiled=True),
        preferred_element_type=jnp.float32,
    )
    query_rows = rotate(query_sum, positions).astype(jnp.bfloat16)
    tree_key_value = jnp.concatenate([rotate(key_sum, positions), value_sum], axis=1).astype(
        jnp.bfloat16
    )
    query_req = query_rows.reshape(local_reqs, DRAFT_TOKENS, query_rows.shape[1])
    key_value_request = tree_key_value.reshape(local_reqs, DRAFT_TOKENS, tree_key_value.shape[1])
    core_count = 2
    plane_count = lax.axis_size("req") // core_count
    place_req = lax.axis_index("req")
    plane_me, core_me = place_req // core_count, place_req % core_count
    plane_order = (plane_me - jnp.arange(plane_count, dtype=jnp.int32)) % plane_count
    out_cols = w_out.shape[1]
    w_out_full = balanced_gather(w_out, plane_count, core_count)
    chunk_count = rows_here // BLOCK_ROWS
    context_all = jax.vmap(attend)(
        query_req, key_value_request, kv_cache, lengths, closure
    ).reshape(rows_here, -1)
    place, weight_hi, weight_lo = slot_tables(routes, gate_weights, CAP)
    outs = []
    for chunk in range(chunk_count):
        rw = slice(chunk * BLOCK_ROWS, (chunk + 1) * BLOCK_ROWS)
        attn_rel = jnp.dot(
            context_all[rw], w_out_full, preferred_element_type=jnp.float32
        ).reshape(BLOCK_ROWS, core_count, plane_count, out_cols)
        attn_rel = jnp.where(core_me == 0, attn_rel, attn_rel[:, ::-1])
        attn_out = (
            jnp.take(attn_rel, plane_order, axis=2).transpose(0, 2, 1, 3).reshape(BLOCK_ROWS, -1)
        )
        residual = (tokens[rw].astype(jnp.float32) + attn_out).astype(jnp.bfloat16)
        moe_in = rms_scale(residual, moe_gain)
        mixed = routed_whole(
            moe_in, place[rw], weight_hi[rw], weight_lo[rw], w_gate, w_up, w_down
        )
        outs.append((residual.astype(jnp.float32) + mixed).astype(jnp.bfloat16))
    layer_out = jnp.concatenate(outs, axis=0)
    new_entries = compact(key_value_request, closure, tree_depth, accepted)
    return (layer_out, new_entries)


def solution(mesh):
    return jax.shard_map(
        local,
        mesh=mesh,
        in_specs=(
            P(("req", "exp"), None),
            P(),
            P("req", None),
            P("req", None),
            P("req", None),
            P(None, "req"),
            P(),
            P("exp", None, None),
            P("exp", None, None),
            P("exp", None, None),
            P(("req", "exp"), None),
            P(("req", "exp"), None),
            P(("req", "exp"), None, None),
            P(("req", "exp")),
            P(("req", "exp"), None),
            P(("req", "exp")),
        ),
        out_specs=(P(("req", "exp"), None), P(("req", "exp"), None, None)),
        check_vma=False,
    )
```

```python
import math

import jax
import jax.numpy as jnp
from jax import lax
from jax.sharding import PartitionSpec as P

QUERY_HEADS = 12
KEY_VALUE_HEADS = 2
HEAD_SIZE = 128
EXPERTS = 32
TOP = 4
DRAFT_TOKENS = 64
CAP = 24
BLOCK_ROWS = 128


eps_norm = 1e-06
rope_base = 1000000.0


def rms_scale(token_rows, gain_vec):
    widened = token_rows.astype(jnp.float32)
    inverse = lax.rsqrt(jnp.mean(widened * widened, axis=-1, keepdims=True) + eps_norm)
    return (widened * inverse * gain_vec).astype(jnp.bfloat16)


def rotate(values, positions):
    row_count = values.shape[0]
    head_count = values.shape[1] // HEAD_SIZE
    half_size = HEAD_SIZE // 2
    reshaped_rows = values.reshape(row_count, head_count, HEAD_SIZE)
    frequency = rope_base ** (-jnp.arange(half_size, dtype=jnp.float32) / half_size)
    angles = positions.astype(jnp.float32)[:, None] * frequency[None, :]
    cosine = jnp.cos(angles)[:, None, :]
    sine_part = jnp.sin(angles)[:, None, :]
    leading = reshaped_rows[..., :half_size]
    second = reshaped_rows[..., half_size:]
    turned = jnp.concatenate(
        [leading * cosine - second * sine_part, second * cosine + leading * sine_part], axis=-1
    )
    return turned.reshape(row_count, head_count * HEAD_SIZE)


def ancestry(parents):
    node_count = parents.shape[-1]
    node_index = jnp.arange(node_count, dtype=jnp.int32)
    parent_step = (parents[..., :, None] == node_index[None, None, :]).astype(jnp.float32)
    closure = jnp.maximum(parent_step, jnp.eye(node_count, dtype=jnp.float32)[None])
    for squaring in range(max(1, (node_count - 1).bit_length())):
        closure = jnp.minimum(jnp.einsum("rij,rjk->rik", closure, closure), 1.0)
    tree_depth = jnp.sum(closure, axis=-1).astype(jnp.int32) - 1
    return (closure, tree_depth)


def attend(query_rows, tree_key_value, cached_row_block, length, closure):
    tree_drafts = query_rows.shape[0]
    queries_per_group = QUERY_HEADS // KEY_VALUE_HEADS
    key_value_width = KEY_VALUE_HEADS * HEAD_SIZE
    reshaped_rows = query_rows.reshape(tree_drafts, KEY_VALUE_HEADS, queries_per_group, HEAD_SIZE)
    cached_key_rows = cached_row_block[:, :key_value_width].reshape(-1, KEY_VALUE_HEADS, HEAD_SIZE)
    cached_value_rows = cached_row_block[:, key_value_width:].reshape(
        -1, KEY_VALUE_HEADS, HEAD_SIZE
    )
    tree_key_rows = tree_key_value[:, :key_value_width].reshape(-1, KEY_VALUE_HEADS, HEAD_SIZE)
    tree_value_rows = tree_key_value[:, key_value_width:].reshape(-1, KEY_VALUE_HEADS, HEAD_SIZE)
    scale = 1.0 / math.sqrt(HEAD_SIZE)
    cache_scores = (
        jnp.einsum(
            "igsd,jgd->gsij", reshaped_rows, cached_key_rows, preferred_element_type=jnp.float32
        )
        * scale
    )
    draft_scores = (
        jnp.einsum(
            "igsd,jgd->gsij", reshaped_rows, tree_key_rows, preferred_element_type=jnp.float32
        )
        * scale
    )
    live_cache = (jnp.arange(cached_row_block.shape[0]) < length)[None, None, None, :]
    live_draft = (closure > 0.5)[None, None, :, :]
    cache_scores = jnp.where(live_cache, cache_scores, -1e30)
    draft_scores = jnp.where(live_draft, draft_scores, -1e30)
    highest = jnp.maximum(jnp.max(cache_scores, axis=-1), jnp.max(draft_scores, axis=-1))[..., None]
    cache_weight = jnp.exp(cache_scores - highest)
    draft_weight = jnp.exp(draft_scores - highest)
    running = jnp.sum(cache_weight, axis=-1, keepdims=True) + jnp.sum(
        draft_weight, axis=-1, keepdims=True
    )
    cache_probs = (cache_weight / running).astype(jnp.bfloat16)
    draft_probs = (draft_weight / running).astype(jnp.bfloat16)
    context = jnp.einsum(
        "gsij,jgd->igsd", cache_probs, cached_value_rows, preferred_element_type=jnp.float32
    )
    context = context + jnp.einsum(
        "gsij,jgd->igsd", draft_probs, tree_value_rows, preferred_element_type=jnp.float32
    )
    return context.reshape(tree_drafts, QUERY_HEADS * HEAD_SIZE).astype(jnp.bfloat16)


def compact(kv_rows, closure, tree_depth, accepted):
    path_mask = jnp.take_along_axis(closure, accepted[:, None, None], axis=1)[:, 0, :]
    level = jnp.arange(kv_rows.shape[1], dtype=jnp.int32)
    select = (
        path_mask[:, None, :] * (tree_depth[:, None, :] == level[None, :, None]).astype(jnp.float32)
    ).astype(jnp.bfloat16)
    return jnp.einsum("rtj,rjw->rtw", select, kv_rows, preferred_element_type=jnp.float32).astype(
        jnp.bfloat16
    )


def slot_tables(routes, gate_weights, capacity):
    rows = routes.shape[0]
    expert_ids = jnp.arange(EXPERTS, dtype=jnp.int32)
    picks = routes[:, :, None] == expert_ids[None, None, :]
    chosen = jnp.sum(picks.astype(jnp.int32), axis=1).astype(jnp.bfloat16)
    row_ids = jnp.arange(rows, dtype=jnp.int32)
    same_block = (row_ids[None, :] // BLOCK_ROWS) == (row_ids[:, None] // BLOCK_ROWS)
    before = ((row_ids[None, :] < row_ids[:, None]) & same_block).astype(jnp.bfloat16)
    earlier = jnp.dot(before, chosen, preferred_element_type=jnp.float32).astype(jnp.int32)
    slot_number = jnp.sum(jnp.where(picks, earlier[:, None, :], 0), axis=2)
    slot_index = routes * capacity + slot_number
    slot_ids = jnp.arange(EXPERTS * capacity, dtype=jnp.int32)
    hit = slot_index[:, :, None] == slot_ids[None, None, :]
    place = jnp.sum(hit.astype(jnp.bfloat16), axis=1)
    weight = jnp.sum(jnp.where(hit, gate_weights[:, :, None], 0.0), axis=1)
    weight_hi = weight.astype(jnp.bfloat16)
    weight_lo = (weight - weight_hi.astype(jnp.float32)).astype(jnp.bfloat16)
    return place, weight_hi, weight_lo


def pack_slots(token_rows, place):
    return jnp.einsum("ts,td->sd", place, token_rows, preferred_element_type=jnp.bfloat16)


def expert_products(received, w_gate, w_up, w_down):
    gate_part = jnp.einsum("pekd,edf->pekf", received, w_gate, preferred_element_type=jnp.float32)
    up_part = jnp.einsum("pekd,edf->pekf", received, w_up, preferred_element_type=jnp.float32)
    hidden = (jnp.maximum(gate_part, 0.0) * up_part).astype(jnp.bfloat16)
    return jnp.einsum("pekf,efd->pekd", hidden, w_down, preferred_element_type=jnp.float32).astype(
        jnp.bfloat16
    )


def combine_picks(returned_rows, weight_hi, weight_lo):
    layer_width = returned_rows.shape[-1]
    rows = weight_hi.shape[0]
    flat_rows = returned_rows.reshape(-1, layer_width)
    both = jnp.concatenate([weight_hi, weight_lo], axis=0)
    mixed = jnp.dot(both, flat_rows, preferred_element_type=jnp.float32)
    return mixed[:rows] + mixed[rows:]


def routed_whole(moe_in, place, weight_hi, weight_lo, w_gate, w_up, w_down):
    capacity = place.shape[1] // EXPERTS
    buffer = pack_slots(moe_in, place)
    peer_count = lax.axis_size("exp")
    reshaped_rows = buffer.reshape(peer_count, w_gate.shape[0], capacity, moe_in.shape[1])
    produced = expert_products(
        lax.all_to_all(reshaped_rows, "exp", split_axis=0, concat_axis=0, tiled=True),
        w_gate,
        w_up,
        w_down,
    )
    returned_rows = lax.all_to_all(produced, "exp", split_axis=0, concat_axis=0, tiled=True)
    return combine_picks(returned_rows, weight_hi, weight_lo)


def local(
    tokens,
    attn_gain,
    w_query,
    key_projection,
    value_projection,
    w_out,
    moe_gain,
    w_gate,
    w_up,
    w_down,
    routes,
    gate_weights,
    kv_cache,
    lengths,
    parents,
    accepted,
):
    rows_here = tokens.shape[0]
    local_reqs = kv_cache.shape[0]
    normed = rms_scale(tokens, attn_gain)
    closure, tree_depth = ancestry(parents)
    positions = (lengths[:, None] + tree_depth).reshape(-1)
    kv_shard = jnp.concatenate([key_projection, value_projection], axis=1)
    peer_count = lax.axis_size("exp")
    place_exp = lax.axis_index("exp")
    out_rows_each = w_out.shape[0] // peer_count
    q_rows_each = w_query.shape[0] // peer_count
    out_slice = lax.dynamic_slice_in_dim(w_out, place_exp * out_rows_each, out_rows_each, axis=0)
    q_slice = lax.dynamic_slice_in_dim(w_query, place_exp * q_rows_each, q_rows_each, axis=0)
    small = lax.all_gather(
        jnp.concatenate([kv_shard.reshape(-1), q_slice.reshape(-1), out_slice.reshape(-1)]),
        "req",
        axis=0,
    )
    req_count = small.shape[0]
    kv_end = kv_shard.size
    q_end = kv_end + q_slice.size
    kv_full = small[:, :kv_end].reshape(req_count * kv_shard.shape[0], kv_shard.shape[1])
    q_rows = small[:, kv_end:q_end].reshape(req_count * q_rows_each, w_query.shape[1])
    out_rows = (
        small[:, q_end:]
        .reshape(req_count, out_rows_each, w_out.shape[1])
        .transpose(1, 0, 2)
        .reshape(out_rows_each, -1)
    )
    q_full = lax.all_gather(q_rows, "exp", axis=0, tiled=True)
    out_rows, q_full = lax.optimization_barrier((out_rows, q_full))
    normed_perm = (
        normed.reshape(rows_here, req_count, peer_count, q_rows_each)
        .transpose(0, 2, 1, 3)
        .reshape(rows_here, -1)
    )
    query_sum = jnp.dot(normed_perm, q_full, preferred_element_type=jnp.float32)
    kv_sum = jnp.dot(normed, kv_full, preferred_element_type=jnp.float32)
    key_sum = kv_sum[:, : key_projection.shape[1]]
    value_sum = kv_sum[:, key_projection.shape[1] :]
    query_rows = rotate(query_sum, positions).astype(jnp.bfloat16)
    tree_key_value = jnp.concatenate([rotate(key_sum, positions), value_sum], axis=1).astype(
        jnp.bfloat16
    )
    query_req = query_rows.reshape(local_reqs, DRAFT_TOKENS, query_rows.shape[1])
    key_value_request = tree_key_value.reshape(local_reqs, DRAFT_TOKENS, tree_key_value.shape[1])
    w_out_full = lax.all_gather(out_rows, "exp", axis=0, tiled=True)
    chunk_count = rows_here // BLOCK_ROWS
    context_all = jax.vmap(attend)(
        query_req, key_value_request, kv_cache, lengths, closure
    ).reshape(rows_here, -1)
    place, weight_hi, weight_lo = slot_tables(routes, gate_weights, CAP)
    outs = []
    for chunk in range(chunk_count):
        rw = slice(chunk * BLOCK_ROWS, (chunk + 1) * BLOCK_ROWS)
        attn_out = jnp.dot(context_all[rw], w_out_full, preferred_element_type=jnp.float32)
        residual = (tokens[rw].astype(jnp.float32) + attn_out).astype(jnp.bfloat16)
        moe_in = rms_scale(residual, moe_gain)
        mixed = routed_whole(
            moe_in, place[rw], weight_hi[rw], weight_lo[rw], w_gate, w_up, w_down
        )
        outs.append((residual.astype(jnp.float32) + mixed).astype(jnp.bfloat16))
    layer_out = jnp.concatenate(outs, axis=0)
    new_entries = compact(key_value_request, closure, tree_depth, accepted)
    return (layer_out, new_entries)


def solution(mesh):
    return jax.shard_map(
        local,
        mesh=mesh,
        in_specs=(
            P(("req", "exp"), None),
            P(),
            P("req", None),
            P("req", None),
            P("req", None),
            P(None, "req"),
            P(),
            P("exp", None, None),
            P("exp", None, None),
            P("exp", None, None),
            P(("req", "exp"), None),
            P(("req", "exp"), None),
            P(("req", "exp"), None, None),
            P(("req", "exp")),
            P(("req", "exp"), None),
            P(("req", "exp")),
        ),
        out_specs=(P(("req", "exp"), None), P(("req", "exp"), None, None)),
        check_vma=False,
    )
```

```python
import math

import jax
import jax.numpy as jnp
from jax import lax
from jax.sharding import PartitionSpec as P

QUERY_HEADS = 12
KEY_VALUE_HEADS = 2
HEAD_SIZE = 128
EXPERTS = 32
TOP = 4
DRAFT_TOKENS = 64
CAP = 24
BLOCK_ROWS = 128


eps_norm = 1e-06
rope_base = 1000000.0


def rms_scale(token_rows, gain_vec):
    widened = token_rows.astype(jnp.float32)
    inverse = lax.rsqrt(jnp.mean(widened * widened, axis=-1, keepdims=True) + eps_norm)
    return (widened * inverse * gain_vec).astype(jnp.bfloat16)


def rotate(values, positions):
    row_count = values.shape[0]
    head_count = values.shape[1] // HEAD_SIZE
    half_size = HEAD_SIZE // 2
    reshaped_rows = values.reshape(row_count, head_count, HEAD_SIZE)
    frequency = rope_base ** (-jnp.arange(half_size, dtype=jnp.float32) / half_size)
    angles = positions.astype(jnp.float32)[:, None] * frequency[None, :]
    cosine = jnp.cos(angles)[:, None, :]
    sine_part = jnp.sin(angles)[:, None, :]
    leading = reshaped_rows[..., :half_size]
    second = reshaped_rows[..., half_size:]
    turned = jnp.concatenate(
        [leading * cosine - second * sine_part, second * cosine + leading * sine_part], axis=-1
    )
    return turned.reshape(row_count, head_count * HEAD_SIZE)


def ancestry(parents):
    node_count = parents.shape[-1]
    node_index = jnp.arange(node_count, dtype=jnp.int32)
    parent_step = (parents[..., :, None] == node_index[None, None, :]).astype(jnp.float32)
    closure = jnp.maximum(parent_step, jnp.eye(node_count, dtype=jnp.float32)[None])
    closure = lax.fori_loop(
        0,
        max(1, (node_count - 1).bit_length()),
        lambda step, held: jnp.minimum(jnp.einsum("rij,rjk->rik", held, held), 1.0),
        closure,
    )
    tree_depth = jnp.sum(closure, axis=-1).astype(jnp.int32) - 1
    return (closure, tree_depth)


def attend(query_rows, tree_key_value, cached_row_block, length, closure):
    tree_drafts = query_rows.shape[0]
    queries_per_group = QUERY_HEADS // KEY_VALUE_HEADS
    key_value_width = KEY_VALUE_HEADS * HEAD_SIZE
    reshaped_rows = query_rows.reshape(tree_drafts, KEY_VALUE_HEADS, queries_per_group, HEAD_SIZE)
    cached_key_rows = cached_row_block[:, :key_value_width].reshape(-1, KEY_VALUE_HEADS, HEAD_SIZE)
    cached_value_rows = cached_row_block[:, key_value_width:].reshape(
        -1, KEY_VALUE_HEADS, HEAD_SIZE
    )
    tree_key_rows = tree_key_value[:, :key_value_width].reshape(-1, KEY_VALUE_HEADS, HEAD_SIZE)
    tree_value_rows = tree_key_value[:, key_value_width:].reshape(-1, KEY_VALUE_HEADS, HEAD_SIZE)
    scale = 1.0 / math.sqrt(HEAD_SIZE)
    cache_scores = (
        jnp.einsum(
            "igsd,jgd->gsij", reshaped_rows, cached_key_rows, preferred_element_type=jnp.float32
        )
        * scale
    )
    draft_scores = (
        jnp.einsum(
            "igsd,jgd->gsij", reshaped_rows, tree_key_rows, preferred_element_type=jnp.float32
        )
        * scale
    )
    live_cache = (jnp.arange(cached_row_block.shape[0]) < length)[None, None, None, :]
    live_draft = (closure > 0.5)[None, None, :, :]
    cache_scores = jnp.where(live_cache, cache_scores, -1e30)
    draft_scores = jnp.where(live_draft, draft_scores, -1e30)
    highest = jnp.maximum(jnp.max(cache_scores, axis=-1), jnp.max(draft_scores, axis=-1))[..., None]
    cache_weight = jnp.exp(cache_scores - highest)
    draft_weight = jnp.exp(draft_scores - highest)
    running = jnp.sum(cache_weight, axis=-1, keepdims=True) + jnp.sum(
        draft_weight, axis=-1, keepdims=True
    )
    cache_probs = (cache_weight / running).astype(jnp.bfloat16)
    draft_probs = (draft_weight / running).astype(jnp.bfloat16)
    context = jnp.einsum(
        "gsij,jgd->igsd", cache_probs, cached_value_rows, preferred_element_type=jnp.float32
    )
    context = context + jnp.einsum(
        "gsij,jgd->igsd", draft_probs, tree_value_rows, preferred_element_type=jnp.float32
    )
    return context.reshape(tree_drafts, QUERY_HEADS * HEAD_SIZE).astype(jnp.bfloat16)


def compact(kv_rows, closure, tree_depth, accepted):
    path_mask = jnp.take_along_axis(closure, accepted[:, None, None], axis=1)[:, 0, :]
    level = jnp.arange(kv_rows.shape[1], dtype=jnp.int32)
    select = (
        path_mask[:, None, :] * (tree_depth[:, None, :] == level[None, :, None]).astype(jnp.float32)
    ).astype(jnp.bfloat16)
    return jnp.einsum("rtj,rjw->rtw", select, kv_rows, preferred_element_type=jnp.float32).astype(
        jnp.bfloat16
    )


def slot_tables(routes, gate_weights, capacity):
    rows = routes.shape[0]
    expert_ids = jnp.arange(EXPERTS, dtype=jnp.int32)
    picks = routes[:, :, None] == expert_ids[None, None, :]
    chosen = jnp.sum(picks.astype(jnp.int32), axis=1).astype(jnp.bfloat16)
    row_ids = jnp.arange(rows, dtype=jnp.int32)
    same_block = (row_ids[None, :] // BLOCK_ROWS) == (row_ids[:, None] // BLOCK_ROWS)
    before = ((row_ids[None, :] < row_ids[:, None]) & same_block).astype(jnp.bfloat16)
    earlier = jnp.dot(before, chosen, preferred_element_type=jnp.float32).astype(jnp.int32)
    slot_number = jnp.sum(jnp.where(picks, earlier[:, None, :], 0), axis=2)
    slot_index = routes * capacity + slot_number
    slot_ids = jnp.arange(EXPERTS * capacity, dtype=jnp.int32)
    hit = slot_index[:, :, None] == slot_ids[None, None, :]
    place = jnp.sum(hit.astype(jnp.bfloat16), axis=1)
    weight = jnp.sum(jnp.where(hit, gate_weights[:, :, None], 0.0), axis=1)
    weight_hi = weight.astype(jnp.bfloat16)
    weight_lo = (weight - weight_hi.astype(jnp.float32)).astype(jnp.bfloat16)
    return place, weight_hi, weight_lo


def pack_slots(token_rows, place):
    return jnp.einsum("ts,td->sd", place, token_rows, preferred_element_type=jnp.bfloat16)


def expert_products(received, w_gate, w_up, w_down):
    gate_part = jnp.einsum("pekd,edf->pekf", received, w_gate, preferred_element_type=jnp.float32)
    up_part = jnp.einsum("pekd,edf->pekf", received, w_up, preferred_element_type=jnp.float32)
    hidden = (jnp.maximum(gate_part, 0.0) * up_part).astype(jnp.bfloat16)
    return jnp.einsum("pekf,efd->pekd", hidden, w_down, preferred_element_type=jnp.float32).astype(
        jnp.bfloat16
    )


def combine_picks(returned_rows, weight_hi, weight_lo):
    layer_width = returned_rows.shape[-1]
    rows = weight_hi.shape[0]
    flat_rows = returned_rows.reshape(-1, layer_width)
    both = jnp.concatenate([weight_hi, weight_lo], axis=0)
    mixed = jnp.dot(both, flat_rows, preferred_element_type=jnp.float32)
    return mixed[:rows] + mixed[rows:]


def routed_whole(buffer, weight_hi, weight_lo, w_gate, w_up, w_down):
    capacity = buffer.shape[0] // EXPERTS
    width = buffer.shape[1]
    peer_count = lax.axis_size("exp")
    reshaped_rows = buffer.reshape(peer_count, w_gate.shape[0], capacity, width)
    produced = expert_products(
        lax.all_to_all(reshaped_rows, "exp", split_axis=0, concat_axis=0, tiled=True),
        w_gate,
        w_up,
        w_down,
    )
    returned_rows = lax.all_to_all(produced, "exp", split_axis=0, concat_axis=0, tiled=True)
    return combine_picks(returned_rows, weight_hi, weight_lo)


def local(
    tokens,
    attn_gain,
    w_query,
    key_projection,
    value_projection,
    w_out,
    moe_gain,
    w_gate,
    w_up,
    w_down,
    routes,
    gate_weights,
    kv_cache,
    lengths,
    parents,
    accepted,
):
    rows_here = tokens.shape[0]
    local_reqs = kv_cache.shape[0]
    normed = rms_scale(tokens, attn_gain)
    closure, tree_depth = ancestry(parents)
    positions = (lengths[:, None] + tree_depth).reshape(-1)
    query_sum = jnp.dot(
        normed,
        lax.all_gather(w_query, "req", axis=0, tiled=True),
        preferred_element_type=jnp.float32,
    )
    key_sum = jnp.dot(
        normed,
        lax.all_gather(key_projection, "req", axis=0, tiled=True),
        preferred_element_type=jnp.float32,
    )
    value_sum = jnp.dot(
        normed,
        lax.all_gather(value_projection, "req", axis=0, tiled=True),
        preferred_element_type=jnp.float32,
    )
    turned = rotate(jnp.concatenate([query_sum, key_sum], axis=1), positions)
    query_rows = turned[:, : query_sum.shape[1]].astype(jnp.bfloat16)
    tree_key_value = jnp.concatenate([turned[:, query_sum.shape[1] :], value_sum], axis=1).astype(
        jnp.bfloat16
    )
    query_req = query_rows.reshape(local_reqs, DRAFT_TOKENS, query_rows.shape[1])
    key_value_request = tree_key_value.reshape(local_reqs, DRAFT_TOKENS, tree_key_value.shape[1])
    w_out_full = lax.all_gather(w_out, "req", axis=1, tiled=True)
    chunk_count = rows_here // BLOCK_ROWS
    context_all = jax.vmap(attend)(
        query_req, key_value_request, kv_cache, lengths, closure
    ).reshape(rows_here, -1)
    place, weight_hi, weight_lo = slot_tables(routes, gate_weights, CAP)
    attn_out = jnp.dot(context_all, w_out_full, preferred_element_type=jnp.float32)
    residual = (tokens.astype(jnp.float32) + attn_out).astype(jnp.bfloat16)
    moe_in = rms_scale(residual, moe_gain)
    buffers = jnp.einsum(
        "hts,htd->hsd",
        place.reshape(chunk_count, BLOCK_ROWS, -1),
        moe_in.reshape(chunk_count, BLOCK_ROWS, -1),
        preferred_element_type=jnp.bfloat16,
    )
    outs = []
    for chunk in range(chunk_count):
        rw = slice(chunk * BLOCK_ROWS, (chunk + 1) * BLOCK_ROWS)
        mixed = routed_whole(buffers[chunk], weight_hi[rw], weight_lo[rw], w_gate, w_up, w_down)
        outs.append(residual[rw].astype(jnp.float32) + mixed)
    layer_out = jnp.concatenate(outs, axis=0).astype(jnp.bfloat16)
    new_entries = compact(key_value_request, closure, tree_depth, accepted)
    return (layer_out, new_entries)


def solution(mesh):
    return jax.shard_map(
        local,
        mesh=mesh,
        in_specs=(
            P(("req", "exp"), None),
            P(),
            P("req", None),
            P("req", None),
            P("req", None),
            P(None, "req"),
            P(),
            P("exp", None, None),
            P("exp", None, None),
            P("exp", None, None),
            P(("req", "exp"), None),
            P(("req", "exp"), None),
            P(("req", "exp"), None, None),
            P(("req", "exp")),
            P(("req", "exp"), None),
            P(("req", "exp")),
        ),
        out_specs=(P(("req", "exp"), None), P(("req", "exp"), None, None)),
        check_vma=False,
    )
```

```python
import math

import jax
import jax.numpy as jnp
from jax import lax
from jax.sharding import PartitionSpec as P

QUERY_HEADS = 12
KEY_VALUE_HEADS = 2
HEAD_SIZE = 128
EXPERTS = 32
TOP = 4
DRAFT_TOKENS = 64
CAP = 24
BLOCK_ROWS = 128


eps_norm = 1e-06
rope_base = 1000000.0


def rms_scale(token_rows, gain_vec):
    widened = token_rows.astype(jnp.float32)
    inverse = lax.rsqrt(jnp.mean(widened * widened, axis=-1, keepdims=True) + eps_norm)
    return (widened * inverse * gain_vec).astype(jnp.bfloat16)


def rotate(values, positions):
    row_count = values.shape[0]
    head_count = values.shape[1] // HEAD_SIZE
    half_size = HEAD_SIZE // 2
    reshaped_rows = values.reshape(row_count, head_count, HEAD_SIZE)
    frequency = rope_base ** (-jnp.arange(half_size, dtype=jnp.float32) / half_size)
    angles = positions.astype(jnp.float32)[:, None] * frequency[None, :]
    cosine = jnp.cos(angles)[:, None, :]
    sine_part = jnp.sin(angles)[:, None, :]
    leading = reshaped_rows[..., :half_size]
    second = reshaped_rows[..., half_size:]
    turned = jnp.concatenate(
        [leading * cosine - second * sine_part, second * cosine + leading * sine_part], axis=-1
    )
    return turned.reshape(row_count, head_count * HEAD_SIZE)


def ancestry(parents):
    node_count = parents.shape[-1]
    node_index = jnp.arange(node_count, dtype=jnp.int32)
    parent_step = (parents[..., :, None] == node_index[None, None, :]).astype(jnp.float32)
    closure = jnp.maximum(parent_step, jnp.eye(node_count, dtype=jnp.float32)[None])
    closure = lax.fori_loop(
        0,
        max(1, (node_count - 1).bit_length()),
        lambda step, held: jnp.minimum(jnp.einsum("rij,rjk->rik", held, held), 1.0),
        closure,
    )
    tree_depth = jnp.sum(closure, axis=-1).astype(jnp.int32) - 1
    return (closure, tree_depth)


def attend(query_rows, tree_key_value, cached_row_block, length, closure):
    tree_drafts = query_rows.shape[0]
    queries_per_group = QUERY_HEADS // KEY_VALUE_HEADS
    key_value_width = KEY_VALUE_HEADS * HEAD_SIZE
    reshaped_rows = query_rows.reshape(tree_drafts, KEY_VALUE_HEADS, queries_per_group, HEAD_SIZE)
    cached_key_rows = cached_row_block[:, :key_value_width].reshape(-1, KEY_VALUE_HEADS, HEAD_SIZE)
    cached_value_rows = cached_row_block[:, key_value_width:].reshape(
        -1, KEY_VALUE_HEADS, HEAD_SIZE
    )
    tree_key_rows = tree_key_value[:, :key_value_width].reshape(-1, KEY_VALUE_HEADS, HEAD_SIZE)
    tree_value_rows = tree_key_value[:, key_value_width:].reshape(-1, KEY_VALUE_HEADS, HEAD_SIZE)
    scale = 1.0 / math.sqrt(HEAD_SIZE)
    cache_scores = (
        jnp.einsum(
            "igsd,jgd->gsij", reshaped_rows, cached_key_rows, preferred_element_type=jnp.float32
        )
        * scale
    )
    draft_scores = (
        jnp.einsum(
            "igsd,jgd->gsij", reshaped_rows, tree_key_rows, preferred_element_type=jnp.float32
        )
        * scale
    )
    live_cache = (jnp.arange(cached_row_block.shape[0]) < length)[None, None, None, :]
    live_draft = (closure > 0.5)[None, None, :, :]
    cache_scores = jnp.where(live_cache, cache_scores, -1e30)
    draft_scores = jnp.where(live_draft, draft_scores, -1e30)
    highest = jnp.maximum(jnp.max(cache_scores, axis=-1), jnp.max(draft_scores, axis=-1))[..., None]
    cache_weight = jnp.exp(cache_scores - highest)
    draft_weight = jnp.exp(draft_scores - highest)
    running = jnp.sum(cache_weight, axis=-1, keepdims=True) + jnp.sum(
        draft_weight, axis=-1, keepdims=True
    )
    cache_probs = (cache_weight / running).astype(jnp.bfloat16)
    draft_probs = (draft_weight / running).astype(jnp.bfloat16)
    context = jnp.einsum(
        "gsij,jgd->igsd", cache_probs, cached_value_rows, preferred_element_type=jnp.float32
    )
    context = context + jnp.einsum(
        "gsij,jgd->igsd", draft_probs, tree_value_rows, preferred_element_type=jnp.float32
    )
    return context.reshape(tree_drafts, QUERY_HEADS * HEAD_SIZE).astype(jnp.bfloat16)


def compact(kv_rows, closure, tree_depth, accepted):
    path_mask = jnp.take_along_axis(closure, accepted[:, None, None], axis=1)[:, 0, :]
    level = jnp.arange(kv_rows.shape[1], dtype=jnp.int32)
    select = (
        path_mask[:, None, :] * (tree_depth[:, None, :] == level[None, :, None]).astype(jnp.float32)
    ).astype(jnp.bfloat16)
    return jnp.einsum("rtj,rjw->rtw", select, kv_rows, preferred_element_type=jnp.float32).astype(
        jnp.bfloat16
    )


def slot_tables(routes, gate_weights, capacity):
    rows = routes.shape[0]
    expert_ids = jnp.arange(EXPERTS, dtype=jnp.int32)
    picks = routes[:, :, None] == expert_ids[None, None, :]
    chosen = jnp.sum(picks.astype(jnp.int32), axis=1).astype(jnp.bfloat16)
    row_ids = jnp.arange(rows, dtype=jnp.int32)
    same_block = (row_ids[None, :] // BLOCK_ROWS) == (row_ids[:, None] // BLOCK_ROWS)
    before = ((row_ids[None, :] < row_ids[:, None]) & same_block).astype(jnp.bfloat16)
    earlier = jnp.dot(before, chosen, preferred_element_type=jnp.float32).astype(jnp.int32)
    slot_number = jnp.sum(jnp.where(picks, earlier[:, None, :], 0), axis=2)
    slot_index = routes * capacity + slot_number
    slot_ids = jnp.arange(EXPERTS * capacity, dtype=jnp.int32)
    hit = slot_index[:, :, None] == slot_ids[None, None, :]
    place = jnp.sum(hit.astype(jnp.bfloat16), axis=1)
    weight = jnp.sum(jnp.where(hit, gate_weights[:, :, None], 0.0), axis=1)
    weight_hi = weight.astype(jnp.bfloat16)
    weight_lo = (weight - weight_hi.astype(jnp.float32)).astype(jnp.bfloat16)
    return place, weight_hi, weight_lo


def pack_slots(token_rows, place):
    return jnp.einsum("ts,td->sd", place, token_rows, preferred_element_type=jnp.bfloat16)


def expert_products(received, w_gate, w_up, w_down):
    gate_part = jnp.einsum("pekd,edf->pekf", received, w_gate, preferred_element_type=jnp.float32)
    up_part = jnp.einsum("pekd,edf->pekf", received, w_up, preferred_element_type=jnp.float32)
    hidden = (jnp.maximum(gate_part, 0.0) * up_part).astype(jnp.bfloat16)
    return jnp.einsum("pekf,efd->pekd", hidden, w_down, preferred_element_type=jnp.float32).astype(
        jnp.bfloat16
    )


def combine_picks(returned_rows, weight_hi, weight_lo):
    layer_width = returned_rows.shape[-1]
    rows = weight_hi.shape[0]
    flat_rows = returned_rows.reshape(-1, layer_width)
    both = jnp.concatenate([weight_hi, weight_lo], axis=0)
    mixed = jnp.dot(both, flat_rows, preferred_element_type=jnp.float32)
    return mixed[:rows] + mixed[rows:]


def routed_whole(moe_in, place, weight_hi, weight_lo, w_gate, w_up, w_down):
    capacity = place.shape[1] // EXPERTS
    buffer = pack_slots(moe_in, place)
    peer_count = lax.axis_size("exp")
    reshaped_rows = buffer.reshape(peer_count, w_gate.shape[0], capacity, moe_in.shape[1])
    produced = expert_products(
        lax.all_to_all(reshaped_rows, "exp", split_axis=0, concat_axis=0, tiled=True),
        w_gate,
        w_up,
        w_down,
    )
    returned_rows = lax.all_to_all(produced, "exp", split_axis=0, concat_axis=0, tiled=True)
    return combine_picks(returned_rows, weight_hi, weight_lo)


def local(
    tokens,
    attn_gain,
    w_query,
    key_projection,
    value_projection,
    w_out,
    moe_gain,
    w_gate,
    w_up,
    w_down,
    routes,
    gate_weights,
    kv_cache,
    lengths,
    parents,
    accepted,
):
    rows_here = tokens.shape[0]
    local_reqs = kv_cache.shape[0]
    normed = rms_scale(tokens, attn_gain)
    closure, tree_depth = ancestry(parents)
    positions = (lengths[:, None] + tree_depth).reshape(-1)
    query_sum = jnp.dot(
        normed,
        lax.all_gather(w_query, "req", axis=0, tiled=True),
        preferred_element_type=jnp.float32,
    )
    key_sum = jnp.dot(
        normed,
        lax.all_gather(key_projection, "req", axis=0, tiled=True),
        preferred_element_type=jnp.float32,
    )
    value_sum = jnp.dot(
        normed,
        lax.all_gather(value_projection, "req", axis=0, tiled=True),
        preferred_element_type=jnp.float32,
    )
    turned = rotate(jnp.concatenate([query_sum, key_sum], axis=1), positions)
    query_rows = turned[:, : query_sum.shape[1]].astype(jnp.bfloat16)
    tree_key_value = jnp.concatenate([turned[:, query_sum.shape[1] :], value_sum], axis=1).astype(
        jnp.bfloat16
    )
    query_req = query_rows.reshape(local_reqs, DRAFT_TOKENS, query_rows.shape[1])
    key_value_request = tree_key_value.reshape(local_reqs, DRAFT_TOKENS, tree_key_value.shape[1])
    w_out_full = lax.all_gather(w_out, "req", axis=1, tiled=True)
    chunk_count = rows_here // BLOCK_ROWS
    context_all = jax.vmap(attend)(
        query_req, key_value_request, kv_cache, lengths, closure
    ).reshape(rows_here, -1)
    place, weight_hi, weight_lo = slot_tables(routes, gate_weights, CAP)
    outs = []
    for chunk in range(chunk_count):
        rw = slice(chunk * BLOCK_ROWS, (chunk + 1) * BLOCK_ROWS)
        attn_out = jnp.dot(context_all[rw], w_out_full, preferred_element_type=jnp.float32)
        residual = (tokens[rw].astype(jnp.float32) + attn_out).astype(jnp.bfloat16)
        moe_in = rms_scale(residual, moe_gain)
        mixed = routed_whole(
            moe_in, place[rw], weight_hi[rw], weight_lo[rw], w_gate, w_up, w_down
        )
        outs.append((residual.astype(jnp.float32) + mixed).astype(jnp.bfloat16))
    layer_out = jnp.concatenate(outs, axis=0)
    new_entries = compact(key_value_request, closure, tree_depth, accepted)
    return (layer_out, new_entries)


def solution(mesh):
    return jax.shard_map(
        local,
        mesh=mesh,
        in_specs=(
            P(("req", "exp"), None),
            P(),
            P("req", None),
            P("req", None),
            P("req", None),
            P(None, "req"),
            P(),
            P("exp", None, None),
            P("exp", None, None),
            P("exp", None, None),
            P(("req", "exp"), None),
            P(("req", "exp"), None),
            P(("req", "exp"), None, None),
            P(("req", "exp")),
            P(("req", "exp"), None),
            P(("req", "exp")),
        ),
        out_specs=(P(("req", "exp"), None), P(("req", "exp"), None, None)),
        check_vma=False,
    )
```

```python
import math

import jax
import jax.numpy as jnp
from jax import lax
from jax.sharding import PartitionSpec as P

QUERY_HEADS = 12
KEY_VALUE_HEADS = 2
HEAD_SIZE = 128
EXPERTS = 32
TOP = 4
DRAFT_TOKENS = 64
CAP = 24
BLOCK_ROWS = 128


eps_norm = 1e-06
rope_base = 1000000.0


def rms_scale(token_rows, gain_vec):
    widened = token_rows.astype(jnp.float32)
    inverse = lax.rsqrt(jnp.mean(widened * widened, axis=-1, keepdims=True) + eps_norm)
    return (widened * inverse * gain_vec).astype(jnp.bfloat16)


def rotate(values, positions):
    row_count = values.shape[0]
    head_count = values.shape[1] // HEAD_SIZE
    half_size = HEAD_SIZE // 2
    reshaped_rows = values.reshape(row_count, head_count, HEAD_SIZE)
    frequency = rope_base ** (-jnp.arange(half_size, dtype=jnp.float32) / half_size)
    angles = positions.astype(jnp.float32)[:, None] * frequency[None, :]
    cosine = jnp.cos(angles)[:, None, :]
    sine_part = jnp.sin(angles)[:, None, :]
    leading = reshaped_rows[..., :half_size]
    second = reshaped_rows[..., half_size:]
    turned = jnp.concatenate(
        [leading * cosine - second * sine_part, second * cosine + leading * sine_part], axis=-1
    )
    return turned.reshape(row_count, head_count * HEAD_SIZE)


def ancestry(parents):
    node_count = parents.shape[-1]
    node_index = jnp.arange(node_count, dtype=jnp.int32)
    parent_step = (parents[..., :, None] == node_index[None, None, :]).astype(jnp.float32)
    closure = jnp.maximum(parent_step, jnp.eye(node_count, dtype=jnp.float32)[None])
    closure = lax.fori_loop(
        0,
        max(1, (node_count - 1).bit_length()),
        lambda step, held: jnp.minimum(jnp.einsum("rij,rjk->rik", held, held), 1.0),
        closure,
    )
    tree_depth = jnp.sum(closure, axis=-1).astype(jnp.int32) - 1
    return (closure, tree_depth)


def attend(query_rows, tree_key_value, cached_row_block, length, closure):
    tree_drafts = query_rows.shape[0]
    queries_per_group = QUERY_HEADS // KEY_VALUE_HEADS
    key_value_width = KEY_VALUE_HEADS * HEAD_SIZE
    reshaped_rows = query_rows.reshape(tree_drafts, KEY_VALUE_HEADS, queries_per_group, HEAD_SIZE)
    cached_key_rows = cached_row_block[:, :key_value_width].reshape(-1, KEY_VALUE_HEADS, HEAD_SIZE)
    cached_value_rows = cached_row_block[:, key_value_width:].reshape(
        -1, KEY_VALUE_HEADS, HEAD_SIZE
    )
    tree_key_rows = tree_key_value[:, :key_value_width].reshape(-1, KEY_VALUE_HEADS, HEAD_SIZE)
    tree_value_rows = tree_key_value[:, key_value_width:].reshape(-1, KEY_VALUE_HEADS, HEAD_SIZE)
    scale = 1.0 / math.sqrt(HEAD_SIZE)
    cache_scores = (
        jnp.einsum(
            "igsd,jgd->gsij", reshaped_rows, cached_key_rows, preferred_element_type=jnp.float32
        )
        * scale
    )
    draft_scores = (
        jnp.einsum(
            "igsd,jgd->gsij", reshaped_rows, tree_key_rows, preferred_element_type=jnp.float32
        )
        * scale
    )
    live_cache = (jnp.arange(cached_row_block.shape[0]) < length)[None, None, None, :]
    live_draft = (closure > 0.5)[None, None, :, :]
    cache_scores = jnp.where(live_cache, cache_scores, -1e30)
    draft_scores = jnp.where(live_draft, draft_scores, -1e30)
    highest = jnp.maximum(jnp.max(cache_scores, axis=-1), jnp.max(draft_scores, axis=-1))[..., None]
    cache_weight = jnp.exp(cache_scores - highest)
    draft_weight = jnp.exp(draft_scores - highest)
    running = jnp.sum(cache_weight, axis=-1, keepdims=True) + jnp.sum(
        draft_weight, axis=-1, keepdims=True
    )
    cache_probs = (cache_weight / running).astype(jnp.bfloat16)
    draft_probs = (draft_weight / running).astype(jnp.bfloat16)
    context = jnp.einsum(
        "gsij,jgd->igsd", cache_probs, cached_value_rows, preferred_element_type=jnp.float32
    )
    context = context + jnp.einsum(
        "gsij,jgd->igsd", draft_probs, tree_value_rows, preferred_element_type=jnp.float32
    )
    return context.reshape(tree_drafts, QUERY_HEADS * HEAD_SIZE).astype(jnp.bfloat16)


def compact(kv_rows, closure, tree_depth, accepted):
    path_mask = jnp.take_along_axis(closure, accepted[:, None, None], axis=1)[:, 0, :]
    level = jnp.arange(kv_rows.shape[1], dtype=jnp.int32)
    select = (
        path_mask[:, None, :] * (tree_depth[:, None, :] == level[None, :, None]).astype(jnp.float32)
    ).astype(jnp.bfloat16)
    return jnp.einsum("rtj,rjw->rtw", select, kv_rows, preferred_element_type=jnp.float32).astype(
        jnp.bfloat16
    )


def slot_tables(routes, gate_weights, capacity):
    rows = routes.shape[0]
    expert_ids = jnp.arange(EXPERTS, dtype=jnp.int32)
    picks = routes[:, :, None] == expert_ids[None, None, :]
    chosen = jnp.sum(picks.astype(jnp.int32), axis=1).astype(jnp.bfloat16)
    row_ids = jnp.arange(rows, dtype=jnp.int32)
    same_block = (row_ids[None, :] // BLOCK_ROWS) == (row_ids[:, None] // BLOCK_ROWS)
    before = ((row_ids[None, :] < row_ids[:, None]) & same_block).astype(jnp.bfloat16)
    earlier = jnp.dot(before, chosen, preferred_element_type=jnp.float32).astype(jnp.int32)
    slot_number = jnp.sum(jnp.where(picks, earlier[:, None, :], 0), axis=2)
    slot_index = routes * capacity + slot_number
    slot_ids = jnp.arange(EXPERTS * capacity, dtype=jnp.int32)
    hit = slot_index[:, :, None] == slot_ids[None, None, :]
    place = jnp.sum(hit.astype(jnp.bfloat16), axis=1)
    weight = jnp.sum(jnp.where(hit, gate_weights[:, :, None], 0.0), axis=1)
    weight_hi = weight.astype(jnp.bfloat16)
    weight_lo = (weight - weight_hi.astype(jnp.float32)).astype(jnp.bfloat16)
    return place, weight_hi, weight_lo


def pack_slots(token_rows, place):
    return jnp.einsum("ts,td->sd", place, token_rows, preferred_element_type=jnp.bfloat16)


def expert_products(received, w_gate, w_up, w_down):
    gate_part = jnp.einsum("pekd,edf->pekf", received, w_gate, preferred_element_type=jnp.float32)
    up_part = jnp.einsum("pekd,edf->pekf", received, w_up, preferred_element_type=jnp.float32)
    hidden = (jnp.maximum(gate_part, 0.0) * up_part).astype(jnp.bfloat16)
    return jnp.einsum("pekf,efd->pekd", hidden, w_down, preferred_element_type=jnp.float32).astype(
        jnp.bfloat16
    )


def combine_picks(returned_rows, weight_hi, weight_lo):
    layer_width = returned_rows.shape[-1]
    rows = weight_hi.shape[0]
    flat_rows = returned_rows.reshape(-1, layer_width)
    both = jnp.concatenate([weight_hi, weight_lo], axis=0)
    mixed = jnp.dot(both, flat_rows, preferred_element_type=jnp.float32)
    return mixed[:rows] + mixed[rows:]


def routed_whole(buffer, weight_hi, weight_lo, w_gate, w_up, w_down):
    capacity = buffer.shape[0] // EXPERTS
    width = buffer.shape[1]
    peer_count = lax.axis_size("exp")
    reshaped_rows = buffer.reshape(peer_count, w_gate.shape[0], capacity, width)
    produced = expert_products(
        lax.all_to_all(reshaped_rows, "exp", split_axis=0, concat_axis=0, tiled=True),
        w_gate,
        w_up,
        w_down,
    )
    returned_rows = lax.all_to_all(produced, "exp", split_axis=0, concat_axis=0, tiled=True)
    return combine_picks(returned_rows, weight_hi, weight_lo)


def local(
    tokens,
    attn_gain,
    w_query,
    key_projection,
    value_projection,
    w_out,
    moe_gain,
    w_gate,
    w_up,
    w_down,
    routes,
    gate_weights,
    kv_cache,
    lengths,
    parents,
    accepted,
):
    rows_here = tokens.shape[0]
    local_reqs = kv_cache.shape[0]
    normed = rms_scale(tokens, attn_gain)
    closure, tree_depth = ancestry(parents)
    positions = (lengths[:, None] + tree_depth).reshape(-1)
    query_sum = jnp.dot(
        normed,
        lax.all_gather(w_query, "req", axis=0, tiled=True),
        preferred_element_type=jnp.float32,
    )
    key_sum = jnp.dot(
        normed,
        lax.all_gather(key_projection, "req", axis=0, tiled=True),
        preferred_element_type=jnp.float32,
    )
    value_sum = jnp.dot(
        normed,
        lax.all_gather(value_projection, "req", axis=0, tiled=True),
        preferred_element_type=jnp.float32,
    )
    turned = rotate(jnp.concatenate([query_sum, key_sum], axis=1), positions)
    query_rows = turned[:, : query_sum.shape[1]].astype(jnp.bfloat16)
    tree_key_value = jnp.concatenate([turned[:, query_sum.shape[1] :], value_sum], axis=1).astype(
        jnp.bfloat16
    )
    query_req = query_rows.reshape(local_reqs, DRAFT_TOKENS, query_rows.shape[1])
    key_value_request = tree_key_value.reshape(local_reqs, DRAFT_TOKENS, tree_key_value.shape[1])
    w_out_full = lax.all_gather(w_out, "req", axis=1, tiled=True)
    chunk_count = rows_here // BLOCK_ROWS
    context_all = jax.vmap(attend)(
        query_req, key_value_request, kv_cache, lengths, closure
    ).reshape(rows_here, -1)
    place, weight_hi, weight_lo = slot_tables(routes, gate_weights, CAP)
    attn_out = jnp.dot(context_all, w_out_full, preferred_element_type=jnp.float32)
    residual = (tokens.astype(jnp.float32) + attn_out).astype(jnp.bfloat16)
    moe_in = rms_scale(residual, moe_gain)
    outs = []
    for chunk in range(chunk_count):
        rw = slice(chunk * BLOCK_ROWS, (chunk + 1) * BLOCK_ROWS)
        buffer = pack_slots(moe_in[rw], place[rw])
        mixed = routed_whole(buffer, weight_hi[rw], weight_lo[rw], w_gate, w_up, w_down)
        outs.append(residual[rw].astype(jnp.float32) + mixed)
    layer_out = jnp.concatenate(outs, axis=0).astype(jnp.bfloat16)
    new_entries = compact(key_value_request, closure, tree_depth, accepted)
    return (layer_out, new_entries)


def solution(mesh):
    return jax.shard_map(
        local,
        mesh=mesh,
        in_specs=(
            P(("req", "exp"), None),
            P(),
            P("req", None),
            P("req", None),
            P("req", None),
            P(None, "req"),
            P(),
            P("exp", None, None),
            P("exp", None, None),
            P("exp", None, None),
            P(("req", "exp"), None),
            P(("req", "exp"), None),
            P(("req", "exp"), None, None),
            P(("req", "exp")),
            P(("req", "exp"), None),
            P(("req", "exp")),
        ),
        out_specs=(P(("req", "exp"), None), P(("req", "exp"), None, None)),
        check_vma=False,
    )
```
